512 devices in a mesh: row: 32 (over z, y_lo), col: 16 (over y_hi, x, core).
Axes of the slice: x: 4, y: 8 (y_hi: 2, y_lo: 4; y = y_hi * 4 + y_lo), z: 8, core: 2. Of those that a mesh axis runs over, the one named last changes fastest.
Arguments:
- group_store: bfloat16 [512, 32, 1600], P('row'), may hold values from -6 to 6
- positions: bfloat16 [320, 1600], replicated, may hold values from -6 to 6
- ln_gain: bfloat16 [1600], replicated, may hold values from 0.099609375 to 1.8984375
- w_query: bfloat16 [1600, 1600], P('row', 'col'), may hold values from -6 to 6
- w_keyval: bfloat16 [1600, 2, 1600], P('row', None, 'col'), may hold values from -6 to 6
- w_out: bfloat16 [1600, 1600], P('col', 'row'), may hold values from -0.3125 to 0.3125
- group_src: int32 [128, 10], replicated, may hold values from 0 to 511, as said below
- lengths: int32 [32, 4], replicated, may hold values from 1 to 10, as said below
- selected: int32 [128, 32], replicated, may hold values from 0 to 319, as said below
Outputs:
- joined_cache: bfloat16 [128, 320, 2, 1600], P('row', None, None, 'col')
- hidden_out: bfloat16 [128, 32, 1600], P('row', None, 'col')
The draws below stay inside these ranges and needn't reach their ends.
Inputs may be any that keep to these rules, and one draw needn't show every extreme that they name: `group_src`: exactly 32 of the 40 entries of the requests of one row device name a group held by another device, and at most 2 of them name any one other device; some device reaches 2 in every draw. `lengths`: every row device has a request with all 10 groups live. `selected`: each row holds 32 distinct places in increasing order, all below 32 times the request's live groups.
All inputs are finite; a program needn't handle non-finite values.
Results may differ from the reference program's by a relative error of at most 0.015.
Values may be sent and summed in bfloat16 or wider, within the bound.
No kernel may reach another device: no remote copies, remote signals or barrier semaphores. Data moves between devices by JAX's collectives and lax.ppermute only.
A program may use at most 64 MiB of HBM per device.

```python
import math
import jax
import jax.numpy as jnp
from jax import lax

D = 1600
HEADS = 25
HEAD_DIM = 64
CH = 32
GROUPS = 10
REQ_DEV = 4
SPAN = 320
SEL = 32
REQUESTS = 128
REM_DEV = 32
CAP = 2
SLOTS = 16
N_ROW = 32


def draw_w_query(key, part):
    own_part = jax.random.normal(jax.random.fold_in(key, 12), (D, D), dtype=jnp.float32) / math.sqrt(D)
    return own_part.astype(jnp.bfloat16)


def draw_w_keyval(key, part):
    key_own = jax.random.normal(jax.random.fold_in(key, 13), (D, D), dtype=jnp.float32) / math.sqrt(D)
    value_own = jax.random.normal(jax.random.fold_in(key, 14), (D, D), dtype=jnp.float32) / math.sqrt(D)
    key_part = key_own
    return jnp.stack([key_part, value_own], axis=1).astype(jnp.bfloat16)


def lengths_table(key):
    base_key = jax.random.fold_in(key, 21)
    owners = REQUESTS // REQ_DEV
    counts = jax.random.randint(jax.random.fold_in(base_key, 1), (owners, REQ_DEV), 1, GROUPS + 1)
    longest = jax.random.randint(jax.random.fold_in(base_key, 2), (owners, 1), 0, REQ_DEV)
    places = jnp.arange(REQ_DEV, dtype=jnp.int32)[None, :]
    return jnp.where(places == longest, GROUPS, counts).astype(jnp.int32)


def draw_lengths(key, part):
    return lengths_table(key)


def draw_selected(key, part):
    live_counts = lengths_table(key).reshape(-1)
    request_keys = jax.random.split(jax.random.fold_in(key, 31), REQUESTS)

    def one_request(request_key, live_count):
        priority = jax.random.permutation(request_key, SPAN).astype(jnp.int32)
        places = jnp.arange(SPAN, dtype=jnp.int32)
        ranking = jnp.where(places < live_count * CH, priority, SPAN + places)
        unused, chosen = lax.top_k(-ranking, SEL)
        return jnp.sort(chosen).astype(jnp.int32)
    return jax.vmap(one_request)(request_keys, live_counts)


def draw_group_src(key, part):
    owners = REQUESTS // REQ_DEV
    ref_count = REQ_DEV * GROUPS
    owner_keys = jax.random.split(jax.random.fold_in(key, 41), owners)

    def one_owner(owner_key, owner):
        priority = jax.random.permutation(jax.random.fold_in(owner_key, 1), ref_count).astype(jnp.int32)
        others = (owner + 1 + jax.random.permutation(jax.random.fold_in(owner_key, 2), owners - 1).astype(jnp.int32)) % owners
        remote = priority < REM_DEV
        which = jnp.minimum(priority // CAP, owners - 2)
        holder = jnp.where(remote, others[which], owner)
        slot = jax.random.randint(jax.random.fold_in(owner_key, 3), (ref_count,), 0, SLOTS)
        return (holder * SLOTS + slot).astype(jnp.int32).reshape(REQ_DEV, GROUPS)
    table = jax.vmap(one_owner)(owner_keys, jnp.arange(owners, dtype=jnp.int32))
    return table.reshape(REQUESTS, GROUPS)


def with_spikes(result, rng, source, target, parts, factor):
    def block_of(dim):
        return (jnp.arange(result.shape[dim]) // (result.shape[dim] // parts)).reshape((-1,) + (1,) * (result.ndim - 1 - dim))

    near = jax.random.permutation(rng, parts)[block_of(target)]
    far = (block_of(target) + parts // 2) % parts
    return jnp.where((block_of(source) == near) | (block_of(source) == far), factor * result, result)


def level_of(stream_key, dims, cuts, least, high):
    level, own = 1.0, jax.random.fold_in(stream_key, 6)
    for dim, blocks in cuts:
        steps = jnp.exp(jax.random.uniform(jax.random.fold_in(own, dim), (blocks,), jnp.float32, least / len(cuts), high / len(cuts)))
        level = level * jnp.repeat(steps, dims[dim] // blocks).reshape([-1 if axis == dim else 1 for axis in range(len(dims))])
    return level


def centred(rng, shape, scale, limit, pieces=(), kind=jnp.bfloat16):
    entries = jax.random.normal(rng, shape, jnp.float32) * scale
    if len(pieces) > 0:
        entries = level_of(rng, shape, pieces, -0.22, 0.18) * entries
    return jnp.clip(entries, min=-limit, max=limit).astype(kind)


def noise_with(stream_key, extent, deviation, bound, pieces, heavy, kind=jnp.bfloat16):
    result = deviation * jax.random.normal(stream_key, extent, jnp.float32)
    if pieces:
        result = result * level_of(stream_key, extent, pieces, -0.22, 0.18)
    return jnp.clip(with_spikes(result, jax.random.fold_in(stream_key, 3), *heavy), -bound, bound).astype(kind)


def setup_inputs(seed: int = 0) -> dict:
    arg_keys = jax.random.split(jax.random.key(seed), 10)
    group_store = centred(arg_keys[0], (N_ROW * SLOTS, CH, D), 1.0, 6.0, ((0, 32),))
    positions = centred(arg_keys[1], (SPAN, D), 1.0, 6.0)
    ln_gain = jnp.clip(1.0 + 0.18 * jax.random.normal(arg_keys[2], (D,), jnp.float32), 0.099609375, 1.8984375).astype(jnp.bfloat16)
    w_query = draw_w_query(jax.random.fold_in(arg_keys[9], 71), 0)
    w_keyval = draw_w_keyval(jax.random.fold_in(arg_keys[9], 71), 0)
    w_out = noise_with(arg_keys[5], (D, D), D ** -0.5, 0.3125, ((0, 16), (1, 32)), (0, 1, 32, 2.75))
    group_src = draw_group_src(jax.random.fold_in(arg_keys[9], 71), 0)
    lengths = draw_lengths(jax.random.fold_in(arg_keys[9], 71), 0)
    selected = draw_selected(jax.random.fold_in(arg_keys[9], 71), 0)
    return {"group_store": group_store, "positions": positions, "ln_gain": ln_gain, "w_query": w_query, "w_keyval": w_keyval, "w_out": w_out, "group_src": group_src, "lengths": lengths, "selected": selected}


def layer_norm(shifted, ln_gain):
    center = shifted - lax.optimization_barrier(jnp.mean(shifted, axis=-1, keepdims=True))
    spread = lax.optimization_barrier(jnp.mean(center * center, axis=-1, keepdims=True))
    return center * lax.rsqrt(spread + 1e-05) * ln_gain.astype(jnp.float32)

def reference(group_store, positions, ln_gain, w_query, w_keyval, w_out, group_src, lengths, selected):
    pos_global = positions.astype(jnp.float32)
    pos_local = jnp.tile(pos_global[:CH], (GROUPS, 1))
    live_groups = lengths.reshape(-1)
    kv_matrix = w_keyval.reshape(D, 2 * D)
    token_place = jnp.arange(SPAN, dtype=jnp.int32)

    def one_request(request):
        cached = group_store[group_src[request]].reshape(SPAN, D)
        shifted = cached.astype(jnp.float32) + pos_global - pos_local
        normed = layer_norm(shifted, ln_gain).astype(jnp.bfloat16)
        keyval = jnp.dot(normed, kv_matrix, preferred_element_type=jnp.float32).astype(jnp.bfloat16).reshape(SPAN, 2, D)
        alive = token_place < live_groups[request] * CH
        keyval = jnp.where(alive[:, None, None], keyval, jnp.zeros_like(keyval))
        picked = selected[request]
        queries = jnp.dot(normed[picked], w_query, preferred_element_type=jnp.float32).astype(jnp.bfloat16)
        query_heads = queries.astype(jnp.float32).reshape(SEL, HEADS, HEAD_DIM)
        key_heads = keyval[:, 0].astype(jnp.float32).reshape(SPAN, HEADS, HEAD_DIM)
        value_heads = keyval[:, 1].astype(jnp.float32).reshape(SPAN, HEADS, HEAD_DIM)
        scores = jnp.einsum('qhe,khe->hqk', query_heads, key_heads) * 0.125
        allowed = token_place[None, :] <= picked[:, None]
        scores = jnp.where(allowed[None], scores, -1e+30)
        highest = lax.optimization_barrier(jnp.max(scores, axis=-1, keepdims=True))
        weights = jnp.where(allowed[None], jnp.exp(scores - highest), 0.0)
        totals = lax.optimization_barrier(jnp.sum(weights, axis=-1))
        summed = jnp.einsum('hqk,khe->hqe', weights, value_heads)
        attended = (summed / totals[:, :, None]).transpose(1, 0, 2).reshape(SEL, D).astype(jnp.bfloat16)
        hidden = shifted[picked] + jnp.dot(attended, w_out, preferred_element_type=jnp.float32)
        return (keyval, hidden.astype(jnp.bfloat16))
    joined_cache, hidden_out = lax.map(one_request, jnp.arange(REQUESTS, dtype=jnp.int32))
    return (joined_cache, hidden_out)
```

```python
import jax
import jax.numpy as jnp
from jax import lax
from jax.sharding import PartitionSpec as P

HEADS = 25
HEAD_DIM = 64
REM_DEV = 32
ROW_RUN = 4
HIGH = lax.Precision.HIGHEST


def layer_norm(shifted, ln_gain):
    center = shifted - jnp.mean(shifted, axis=-1, keepdims=True)
    spread = jnp.mean(center * center, axis=-1, keepdims=True)
    return center * lax.rsqrt(spread + 1e-05) * ln_gain.astype(jnp.float32)


def row_gather(block, row_count):
    run = ROW_RUN if row_count % ROW_RUN == 0 else 1
    runs = row_count // run
    inner = [block] + [
        lax.ppermute(block, "row", [(z * run + a, z * run + (a + s) % run) for z in range(runs) for a in range(run)])
        for s in range(1, run)
    ]
    stage = jnp.stack(inner)
    outer = [stage] + [
        lax.ppermute(stage, "row", [(z * run + a, ((z + s) % runs) * run + a) for z in range(runs) for a in range(run)])
        for s in range(1, runs)
    ]
    stacked = jnp.stack(outer)
    me = lax.axis_index("row")
    z, a = me // run, me % run
    src_z = (z - jnp.arange(runs)) % runs
    src_a = (a - jnp.arange(run)) % run
    order_z = jnp.argsort(src_z)
    order_a = jnp.argsort(src_a)
    ordered = stacked[order_z][:, order_a]
    return ordered.reshape((row_count,) + block.shape)


def gather_weights(w_query, w_keyval, w_out, row_count):
    q_rows, q_cols = w_query.shape
    o_rows, o_cols = w_out.shape
    pack = jnp.concatenate([w_query.reshape(-1), w_keyval.reshape(-1), w_out.reshape(-1)])
    allw = row_gather(pack, row_count)
    q_size = w_query.size
    kv_size = w_keyval.size
    query_rows = allw[:, :q_size].reshape(row_count * q_rows, q_cols)
    keyval_rows = allw[:, q_size:q_size + kv_size].reshape(row_count * q_rows, 2, q_cols)
    out_cols = (
        allw[:, q_size + kv_size:]
        .reshape(row_count, o_rows, o_cols)
        .transpose(1, 0, 2)
        .reshape(o_rows, row_count * o_cols)
    )
    return query_rows, keyval_rows, out_cols


def fetch_groups(group_store, group_src, row_count, row_index, req_here):
    slot_count = group_store.shape[0]
    group_count = group_src.shape[1]
    ref_count = req_here * group_count
    capacity = max(2, (REM_DEV + row_count - 2) // (row_count - 1))
    owner_src = group_src.reshape(row_count, ref_count)
    holder_all = owner_src // slot_count
    slot_all = owner_src % slot_count
    owner_ids = jnp.arange(row_count, dtype=jnp.int32)
    remote_all = holder_all != owner_ids[:, None]
    outgoing = remote_all & (holder_all == row_index)
    out_rank = jnp.cumsum(outgoing.astype(jnp.int32), axis=1) - 1
    slot_ids = jnp.arange(capacity, dtype=jnp.int32)
    chosen = outgoing[:, None, :] & (out_rank[:, None, :] == slot_ids[None, :, None])
    send_slot = jnp.sum(jnp.where(chosen, slot_all[:, None, :], 0), axis=2)
    send_live = jnp.any(chosen, axis=2)
    my_holder = lax.dynamic_index_in_dim(holder_all, row_index, 0, keepdims=False)
    my_slot = lax.dynamic_index_in_dim(slot_all, row_index, 0, keepdims=False)
    my_remote = lax.dynamic_index_in_dim(remote_all, row_index, 0, keepdims=False)
    incoming = (my_holder[None, :] == owner_ids[:, None]) & my_remote[None, :]
    in_rank = jnp.cumsum(incoming.astype(jnp.int32), axis=1) - 1
    my_rank = jnp.sum(jnp.where(incoming, in_rank, 0), axis=0)
    flat_index = my_holder * capacity + my_rank
    payload = group_store[send_slot]
    received = lax.all_to_all(
        jnp.where(send_live[:, :, None, None], payload, jnp.zeros_like(payload)),
        "row",
        split_axis=0,
        concat_axis=0,
        tiled=True,
    )
    flat = received.reshape((row_count * capacity,) + group_store.shape[1:])
    far = flat[jnp.where(my_remote, flat_index, 0)]
    near = group_store[my_slot]
    return jnp.where(my_remote[:, None, None], far, near)


def per_device(
    group_store, positions, ln_gain, w_query, w_keyval, w_out, group_src, lengths, selected
):
    row_count = lax.axis_size("row")
    col_count = lax.axis_size("col")
    row_index = lax.axis_index("row")
    col_index = lax.axis_index("col")
    slot_count, group_len, full_width = group_store.shape
    narrow = full_width // col_count
    req_here = lengths.shape[1]
    group_count = group_src.shape[1]
    token_span = group_count * group_len
    sel_count = selected.shape[1]
    query_count = req_here * sel_count

    query_rows, keyval_rows, out_cols = gather_weights(w_query, w_keyval, w_out, row_count)
    groups = fetch_groups(group_store, group_src, row_count, row_index, req_here)

    pos_global = positions.astype(jnp.float32)
    pos_local = jnp.tile(pos_global[:group_len], (group_count, 1))
    cached = groups.reshape(req_here, token_span, full_width)
    shifted = cached.astype(jnp.float32) + pos_global - pos_local
    normed = layer_norm(shifted, ln_gain).astype(jnp.bfloat16)

    my_lengths = lax.dynamic_index_in_dim(lengths, row_index, 0, keepdims=False)
    my_picked = lax.dynamic_slice_in_dim(selected, row_index * req_here, req_here, 0)
    token_place = jnp.arange(token_span, dtype=jnp.int32)

    keyval = jnp.einsum(
        "btd,dsc->btsc", normed, keyval_rows, preferred_element_type=jnp.float32
    ).astype(jnp.bfloat16)
    alive = token_place[None, :] < (my_lengths * group_len)[:, None]
    joined_cache = jnp.where(alive[:, :, None, None], keyval, jnp.zeros_like(keyval))

    req_ids = jnp.arange(req_here, dtype=jnp.int32)[:, None]
    picked_norm = normed[req_ids, my_picked]
    queries = jnp.einsum(
        "bid,dc->bic", picked_norm, query_rows, preferred_element_type=jnp.float32
    ).astype(jnp.bfloat16)

    first_feature = col_index * narrow
    feature_head = (first_feature + jnp.arange(narrow, dtype=jnp.int32)) // HEAD_DIM
    first_head = first_feature // HEAD_DIM
    last_piece = (first_feature + narrow - 1) // HEAD_DIM - first_head
    piece_count = (narrow + 2 * HEAD_DIM - 2) // HEAD_DIM
    query_f = queries.astype(jnp.float32)
    key_f = joined_cache[:, :, 0].astype(jnp.float32)
    value_f = joined_cache[:, :, 1].astype(jnp.float32)
    masks = [feature_head == first_head + p for p in range(piece_count)]
    partial = [
        jnp.einsum(
            "bie,bte->bit", jnp.where(m[None, None, :], query_f, 0.0), key_f, precision=HIGH
        )
        for m in masks
    ]
    right_piece = partial[0]
    for p in range(1, piece_count):
        right_piece = jnp.where(last_piece == p, partial[p], right_piece)
    from_left = lax.ppermute(right_piece, "col", [(i, i + 1) for i in range(col_count - 1)])
    from_right = lax.ppermute(partial[0], "col", [(i + 1, i) for i in range(col_count - 1)])
    allowed = token_place[None, None, :] <= my_picked[:, :, None]
    attended = jnp.zeros((req_here, sel_count, narrow), jnp.float32)
    for p in range(piece_count):
        full = partial[p]
        if p == 0:
            full = full + from_left
        full = full + jnp.where(last_piece == p, from_right, 0.0)
        scores = jnp.where(allowed, full * 0.125, -1e30)
        highest = jnp.max(scores, axis=-1, keepdims=True)
        weights = jnp.where(allowed, jnp.exp(scores - highest), 0.0)
        totals = jnp.sum(weights, axis=-1)
        summed = jnp.einsum("bit,bte->bie", weights, value_f, precision=HIGH)
        attended = jnp.where(masks[p][None, None, :], summed / totals[:, :, None], attended)
    attended = attended.astype(jnp.bfloat16).reshape(query_count, narrow)

    projected = jnp.dot(attended, out_cols, preferred_element_type=jnp.float32)
    projected = projected.reshape(query_count, col_count, narrow).transpose(1, 0, 2)
    own_out = jnp.sum(lax.all_to_all(projected, "col", 0, 0, tiled=True), axis=0)
    picked_shift = shifted[req_ids, my_picked]
    own_shift = lax.dynamic_slice_in_dim(
        picked_shift.reshape(query_count, full_width), first_feature, narrow, 1
    )
    hidden_out = (own_shift + own_out).astype(jnp.bfloat16).reshape(req_here, sel_count, narrow)
    return (joined_cache, hidden_out)


def solution(mesh):
    return jax.shard_map(
        per_device,
        mesh=mesh,
        in_specs=(
            P("row", None, None),
            P(),
            P(),
            P("row", "col"),
            P("row", None, "col"),
            P("col", "row"),
            P(),
            P(),
            P(),
        ),
        out_specs=(P("row", None, None, "col"), P("row", None, "col")),
        check_vma=False,
    )
```

```python
import jax
import jax.numpy as jnp
from jax import lax
from jax.sharding import PartitionSpec as P

HEADS = 25
HEAD_DIM = 64
REM_DEV = 32
ROW_RUN = 4
FEATURE_SPLIT = 4
HIGH = lax.Precision.HIGHEST


def layer_norm(shifted, ln_gain):
    center = shifted - jnp.mean(shifted, axis=-1, keepdims=True)
    spread = jnp.mean(center * center, axis=-1, keepdims=True)
    return center * lax.rsqrt(spread + 1e-05) * ln_gain.astype(jnp.float32)


def row_gather(block, row_count):
    run = ROW_RUN if row_count % ROW_RUN == 0 else 1
    runs = row_count // run
    inner = [block] + [
        lax.ppermute(block, "row", [(z * run + a, z * run + (a + s) % run) for z in range(runs) for a in range(run)])
        for s in range(1, run)
    ]
    stage = jnp.stack(inner)
    outer = [stage] + [
        lax.ppermute(stage, "row", [(z * run + a, ((z + s) % runs) * run + a) for z in range(runs) for a in range(run)])
        for s in range(1, runs)
    ]
    stacked = jnp.stack(outer)
    me = lax.axis_index("row")
    z, a = me // run, me % run
    src_z = (z - jnp.arange(runs)) % runs
    src_a = (a - jnp.arange(run)) % run
    order_z = jnp.argsort(src_z)
    order_a = jnp.argsort(src_a)
    ordered = stacked[order_z][:, order_a]
    return ordered.reshape((row_count,) + block.shape)


def gather_weights(w_query, w_keyval, w_out, row_count):
    q_rows, q_cols = w_query.shape
    o_rows, o_cols = w_out.shape
    pack = jnp.concatenate([w_query.reshape(-1), w_keyval.reshape(-1), w_out.reshape(-1)])
    allw = row_gather(pack, row_count)
    q_size = w_query.size
    kv_size = w_keyval.size
    query_rows = allw[:, :q_size].reshape(row_count * q_rows, q_cols)
    keyval_rows = allw[:, q_size:q_size + kv_size].reshape(row_count * q_rows, 2, q_cols)
    out_cols = (
        allw[:, q_size + kv_size:]
        .reshape(row_count, o_rows, o_cols)
        .transpose(1, 0, 2)
        .reshape(o_rows, row_count * o_cols)
    )
    return query_rows, keyval_rows, out_cols


def fetch_groups(group_store, group_src, row_count, row_index, col_count, col_index, req_here):
    slot_count, group_len, full_width = group_store.shape
    group_count = group_src.shape[1]
    ref_count = req_here * group_count
    capacity = max(2, (REM_DEV + row_count - 2) // (row_count - 1))
    owner_src = group_src.reshape(row_count, ref_count)
    holder_all = owner_src // slot_count
    slot_all = owner_src % slot_count
    owner_ids = jnp.arange(row_count, dtype=jnp.int32)
    remote_all = holder_all != owner_ids[:, None]
    outgoing = remote_all & (holder_all == row_index)
    out_rank = jnp.cumsum(outgoing.astype(jnp.int32), axis=1) - 1
    slot_ids = jnp.arange(capacity, dtype=jnp.int32)
    chosen = outgoing[:, None, :] & (out_rank[:, None, :] == slot_ids[None, :, None])
    send_slot = jnp.sum(jnp.where(chosen, slot_all[:, None, :], 0), axis=2)
    send_live = jnp.any(chosen, axis=2)
    my_holder = lax.dynamic_index_in_dim(holder_all, row_index, 0, keepdims=False)
    my_slot = lax.dynamic_index_in_dim(slot_all, row_index, 0, keepdims=False)
    my_remote = lax.dynamic_index_in_dim(remote_all, row_index, 0, keepdims=False)
    incoming = (my_holder[None, :] == owner_ids[:, None]) & my_remote[None, :]
    in_rank = jnp.cumsum(incoming.astype(jnp.int32), axis=1) - 1
    my_rank = jnp.sum(jnp.where(incoming, in_rank, 0), axis=0)
    flat_index = my_holder * capacity + my_rank
    ordinal = jnp.cumsum(my_remote.astype(jnp.int32)) - 1
    compact_ids = jnp.arange(REM_DEV, dtype=jnp.int32)
    compact_pick = my_remote[None, :] & (ordinal[None, :] == compact_ids[:, None])
    compact_index = jnp.sum(jnp.where(compact_pick, flat_index[None, :], 0), axis=1)

    split = FEATURE_SPLIT
    if col_count % split or full_width % split:
        split = 1
    part = full_width // split
    own_part = col_index % split
    store_parts = group_store.reshape(slot_count, group_len, split, part)
    my_store = lax.dynamic_index_in_dim(store_parts, own_part, 2, keepdims=False)
    payload = my_store[send_slot]
    received = lax.all_to_all(
        jnp.where(send_live[:, :, None, None], payload, jnp.zeros_like(payload)),
        "row",
        split_axis=0,
        concat_axis=0,
        tiled=True,
    )
    flat = received.reshape(row_count * capacity, group_len, part)
    compact = flat[compact_index]
    pieces = [compact] + [
        lax.ppermute(compact, "col", [(c, c ^ m) for c in range(col_count)]) for m in range(1, split)
    ]
    stacked = jnp.stack(pieces)[jnp.arange(split, dtype=jnp.int32) ^ own_part]
    far_all = stacked.transpose(1, 2, 0, 3).reshape(REM_DEV, group_len, full_width)
    far = far_all[jnp.clip(ordinal, 0, REM_DEV - 1)]
    near = group_store[my_slot]
    return jnp.where(my_remote[:, None, None], far, near)


def per_device(
    group_store, positions, ln_gain, w_query, w_keyval, w_out, group_src, lengths, selected
):
    row_count = lax.axis_size("row")
    col_count = lax.axis_size("col")
    row_index = lax.axis_index("row")
    col_index = lax.axis_index("col")
    slot_count, group_len, full_width = group_store.shape
    narrow = full_width // col_count
    req_here = lengths.shape[1]
    group_count = group_src.shape[1]
    token_span = group_count * group_len
    sel_count = selected.shape[1]
    query_count = req_here * sel_count

    query_rows, keyval_rows, out_cols = gather_weights(w_query, w_keyval, w_out, row_count)
    groups = fetch_groups(
        group_store, group_src, row_count, row_index, col_count, col_index, req_here
    )

    pos_global = positions.astype(jnp.float32)
    pos_local = jnp.tile(pos_global[:group_len], (group_count, 1))
    cached = groups.reshape(req_here, token_span, full_width)
    shifted = cached.astype(jnp.float32) + pos_global - pos_local
    normed = layer_norm(shifted, ln_gain).astype(jnp.bfloat16)

    my_lengths = lax.dynamic_index_in_dim(lengths, row_index, 0, keepdims=False)
    my_picked = lax.dynamic_slice_in_dim(selected, row_index * req_here, req_here, 0)
    token_place = jnp.arange(token_span, dtype=jnp.int32)

    keyval = jnp.einsum(
        "btd,dsc->btsc", normed, keyval_rows, preferred_element_type=jnp.float32
    ).astype(jnp.bfloat16)
    alive = token_place[None, :] < (my_lengths * group_len)[:, None]
    joined_cache = jnp.where(alive[:, :, None, None], keyval, jnp.zeros_like(keyval))

    req_ids = jnp.arange(req_here, dtype=jnp.int32)[:, None]
    picked_norm = normed[req_ids, my_picked]
    queries = jnp.einsum(
        "bid,dc->bic", picked_norm, query_rows, preferred_element_type=jnp.float32
    ).astype(jnp.bfloat16)

    first_feature = col_index * narrow
    feature_head = (first_feature + jnp.arange(narrow, dtype=jnp.int32)) // HEAD_DIM
    first_head = first_feature // HEAD_DIM
    last_piece = (first_feature + narrow - 1) // HEAD_DIM - first_head
    piece_count = (narrow + 2 * HEAD_DIM - 2) // HEAD_DIM
    query_f = queries.astype(jnp.float32)
    key_f = joined_cache[:, :, 0].astype(jnp.float32)
    value_f = joined_cache[:, :, 1].astype(jnp.float32)
    masks = [feature_head == first_head + p for p in range(piece_count)]
    partial = [
        jnp.einsum(
            "bie,bte->bit", jnp.where(m[None, None, :], query_f, 0.0), key_f, precision=HIGH
        )
        for m in masks
    ]
    right_piece = partial[0]
    for p in range(1, piece_count):
        right_piece = jnp.where(last_piece == p, partial[p], right_piece)
    from_left = lax.ppermute(right_piece, "col", [(i, i + 1) for i in range(col_count - 1)])
    from_right = lax.ppermute(partial[0], "col", [(i + 1, i) for i in range(col_count - 1)])
    allowed = token_place[None, None, :] <= my_picked[:, :, None]
    attended = jnp.zeros((req_here, sel_count, narrow), jnp.float32)
    for p in range(piece_count):
        full = partial[p]
        if p == 0:
            full = full + from_left
        full = full + jnp.where(last_piece == p, from_right, 0.0)
        scores = jnp.where(allowed, full * 0.125, -1e30)
        highest = jnp.max(scores, axis=-1, keepdims=True)
        weights = jnp.where(allowed, jnp.exp(scores - highest), 0.0)
        totals = jnp.sum(weights, axis=-1)
        summed = jnp.einsum("bit,bte->bie", weights, value_f, precision=HIGH)
        attended = jnp.where(masks[p][None, None, :], summed / totals[:, :, None], attended)
    attended = attended.astype(jnp.bfloat16).reshape(query_count, narrow)

    projected = jnp.dot(attended, out_cols, preferred_element_type=jnp.float32)
    projected = projected.reshape(query_count, col_count, narrow).transpose(1, 0, 2)
    own_out = jnp.sum(lax.all_to_all(projected, "col", 0, 0, tiled=True), axis=0)
    picked_shift = shifted[req_ids, my_picked]
    own_shift = lax.dynamic_slice_in_dim(
        picked_shift.reshape(query_count, full_width), first_feature, narrow, 1
    )
    hidden_out = (own_shift + own_out).astype(jnp.bfloat16).reshape(req_here, sel_count, narrow)
    return (joined_cache, hidden_out)


def solution(mesh):
    return jax.shard_map(
        per_device,
        mesh=mesh,
        in_specs=(
            P("row", None, None),
            P(),
            P(),
            P("row", "col"),
            P("row", None, "col"),
            P("col", "row"),
            P(),
            P(),
            P(),
        ),
        out_specs=(P("row", None, None, "col"), P("row", None, "col")),
        check_vma=False,
    )
```

```python
import jax
import jax.numpy as jnp
from jax import lax
from jax.sharding import PartitionSpec as P

HEADS = 25
HEAD_DIM = 64
REM_DEV = 32
ROW_RUN = 4
FEATURE_SPLIT = 2
HIGH = lax.Precision.HIGHEST


def layer_norm(shifted, ln_gain):
    center = shifted - jnp.mean(shifted, axis=-1, keepdims=True)
    spread = jnp.mean(center * center, axis=-1, keepdims=True)
    return center * lax.rsqrt(spread + 1e-05) * ln_gain.astype(jnp.float32)


def row_gather(block, row_count):
    run = ROW_RUN if row_count % ROW_RUN == 0 else 1
    runs = row_count // run
    inner = [block] + [
        lax.ppermute(block, "row", [(z * run + a, z * run + (a + s) % run) for z in range(runs) for a in range(run)])
        for s in range(1, run)
    ]
    stage = jnp.stack(inner)
    outer = [stage] + [
        lax.ppermute(stage, "row", [(z * run + a, ((z + s) % runs) * run + a) for z in range(runs) for a in range(run)])
        for s in range(1, runs)
    ]
    stacked = jnp.stack(outer)
    me = lax.axis_index("row")
    z, a = me // run, me % run
    src_z = (z - jnp.arange(runs)) % runs
    src_a = (a - jnp.arange(run)) % run
    order_z = jnp.argsort(src_z)
    order_a = jnp.argsort(src_a)
    ordered = stacked[order_z][:, order_a]
    return ordered.reshape((row_count,) + block.shape)


def gather_weights(w_query, w_keyval, w_out, row_count):
    q_rows, q_cols = w_query.shape
    o_rows, o_cols = w_out.shape
    pack = jnp.concatenate([w_query.reshape(-1), w_keyval.reshape(-1), w_out.reshape(-1)])
    allw = row_gather(pack, row_count)
    q_size = w_query.size
    kv_size = w_keyval.size
    query_rows = allw[:, :q_size].reshape(row_count * q_rows, q_cols)
    keyval_rows = allw[:, q_size:q_size + kv_size].reshape(row_count * q_rows, 2, q_cols)
    out_cols = (
        allw[:, q_size + kv_size:]
        .reshape(row_count, o_rows, o_cols)
        .transpose(1, 0, 2)
        .reshape(o_rows, row_count * o_cols)
    )
    return query_rows, keyval_rows, out_cols


def fetch_groups(group_store, group_src, row_count, row_index, col_count, col_index, req_here):
    slot_count, group_len, full_width = group_store.shape
    group_count = group_src.shape[1]
    ref_count = req_here * group_count
    capacity = max(2, (REM_DEV + row_count - 2) // (row_count - 1))
    owner_src = group_src.reshape(row_count, ref_count)
    holder_all = owner_src // slot_count
    slot_all = owner_src % slot_count
    owner_ids = jnp.arange(row_count, dtype=jnp.int32)
    remote_all = holder_all != owner_ids[:, None]
    outgoing = remote_all & (holder_all == row_index)
    out_rank = jnp.cumsum(outgoing.astype(jnp.int32), axis=1) - 1
    slot_ids = jnp.arange(capacity, dtype=jnp.int32)
    chosen = outgoing[:, None, :] & (out_rank[:, None, :] == slot_ids[None, :, None])
    send_slot = jnp.sum(jnp.where(chosen, slot_all[:, None, :], 0), axis=2)
    send_live = jnp.any(chosen, axis=2)
    my_holder = lax.dynamic_index_in_dim(holder_all, row_index, 0, keepdims=False)
    my_slot = lax.dynamic_index_in_dim(slot_all, row_index, 0, keepdims=False)
    my_remote = lax.dynamic_index_in_dim(remote_all, row_index, 0, keepdims=False)
    incoming = (my_holder[None, :] == owner_ids[:, None]) & my_remote[None, :]
    in_rank = jnp.cumsum(incoming.astype(jnp.int32), axis=1) - 1
    my_rank = jnp.sum(jnp.where(incoming, in_rank, 0), axis=0)
    flat_index = my_holder * capacity + my_rank
    ordinal = jnp.cumsum(my_remote.astype(jnp.int32)) - 1
    compact_ids = jnp.arange(REM_DEV, dtype=jnp.int32)
    compact_pick = my_remote[None, :] & (ordinal[None, :] == compact_ids[:, None])
    compact_index = jnp.sum(jnp.where(compact_pick, flat_index[None, :], 0), axis=1)

    split = FEATURE_SPLIT
    if col_count % split or full_width % split:
        split = 1
    part = full_width // split
    own_part = col_index % split
    store_parts = group_store.reshape(slot_count, group_len, split, part)
    my_store = lax.dynamic_index_in_dim(store_parts, own_part, 2, keepdims=False)
    payload = my_store[send_slot]
    received = lax.all_to_all(
        jnp.where(send_live[:, :, None, None], payload, jnp.zeros_like(payload)),
        "row",
        split_axis=0,
        concat_axis=0,
        tiled=True,
    )
    flat = received.reshape(row_count * capacity, group_len, part)
    compact = flat[compact_index]
    pieces = [compact] + [
        lax.ppermute(compact, "col", [(c, c ^ m) for c in range(col_count)]) for m in range(1, split)
    ]
    stacked = jnp.stack(pieces)[jnp.arange(split, dtype=jnp.int32) ^ own_part]
    far_all = stacked.transpose(1, 2, 0, 3).reshape(REM_DEV, group_len, full_width)
    far = far_all[jnp.clip(ordinal, 0, REM_DEV - 1)]
    near = group_store[my_slot]
    return jnp.where(my_remote[:, None, None], far, near)


def per_device(
    group_store, positions, ln_gain, w_query, w_keyval, w_out, group_src, lengths, selected
):
    row_count = lax.axis_size("row")
    col_count = lax.axis_size("col")
    row_index = lax.axis_index("row")
    col_index = lax.axis_index("col")
    slot_count, group_len, full_width = group_store.shape
    narrow = full_width // col_count
    req_here = lengths.shape[1]
    group_count = group_src.shape[1]
    token_span = group_count * group_len
    sel_count = selected.shape[1]
    query_count = req_here * sel_count

    query_rows, keyval_rows, out_cols = gather_weights(w_query, w_keyval, w_out, row_count)
    groups = fetch_groups(
        group_store, group_src, row_count, row_index, col_count, col_index, req_here
    )

    pos_global = positions.astype(jnp.float32)
    pos_local = jnp.tile(pos_global[:group_len], (group_count, 1))
    cached = groups.reshape(req_here, token_span, full_width)
    shifted = cached.astype(jnp.float32) + pos_global - pos_local
    normed = layer_norm(shifted, ln_gain).astype(jnp.bfloat16)

    my_lengths = lax.dynamic_index_in_dim(lengths, row_index, 0, keepdims=False)
    my_picked = lax.dynamic_slice_in_dim(selected, row_index * req_here, req_here, 0)
    token_place = jnp.arange(token_span, dtype=jnp.int32)

    keyval = jnp.einsum(
        "btd,dsc->btsc", normed, keyval_rows, preferred_element_type=jnp.float32
    ).astype(jnp.bfloat16)
    alive = token_place[None, :] < (my_lengths * group_len)[:, None]
    joined_cache = jnp.where(alive[:, :, None, None], keyval, jnp.zeros_like(keyval))

    req_ids = jnp.arange(req_here, dtype=jnp.int32)[:, None]
    picked_norm = normed[req_ids, my_picked]
    queries = jnp.einsum(
        "bid,dc->bic", picked_norm, query_rows, preferred_element_type=jnp.float32
    ).astype(jnp.bfloat16)

    first_feature = col_index * narrow
    feature_head = (first_feature + jnp.arange(narrow, dtype=jnp.int32)) // HEAD_DIM
    first_head = first_feature // HEAD_DIM
    last_piece = (first_feature + narrow - 1) // HEAD_DIM - first_head
    piece_count = (narrow + 2 * HEAD_DIM - 2) // HEAD_DIM
    query_f = queries.astype(jnp.float32)
    key_f = joined_cache[:, :, 0].astype(jnp.float32)
    value_f = joined_cache[:, :, 1].astype(jnp.float32)
    masks = [feature_head == first_head + p for p in range(piece_count)]
    partial = [
        jnp.einsum(
            "bie,bte->bit", jnp.where(m[None, None, :], query_f, 0.0), key_f, precision=HIGH
        )
        for m in masks
    ]
    right_piece = partial[0]
    for p in range(1, piece_count):
        right_piece = jnp.where(last_piece == p, partial[p], right_piece)
    from_left = lax.ppermute(right_piece, "col", [(i, i + 1) for i in range(col_count - 1)])
    from_right = lax.ppermute(partial[0], "col", [(i + 1, i) for i in range(col_count - 1)])
    allowed = token_place[None, None, :] <= my_picked[:, :, None]
    attended = jnp.zeros((req_here, sel_count, narrow), jnp.float32)
    for p in range(piece_count):
        full = partial[p]
        if p == 0:
            full = full + from_left
        full = full + jnp.where(last_piece == p, from_right, 0.0)
        scores = jnp.where(allowed, full * 0.125, -1e30)
        highest = jnp.max(scores, axis=-1, keepdims=True)
        weights = jnp.where(allowed, jnp.exp(scores - highest), 0.0)
        totals = jnp.sum(weights, axis=-1)
        summed = jnp.einsum("bit,bte->bie", weights, value_f, precision=HIGH)
        attended = jnp.where(masks[p][None, None, :], summed / totals[:, :, None], attended)
    attended = attended.astype(jnp.bfloat16).reshape(query_count, narrow)

    projected = jnp.dot(attended, out_cols, preferred_element_type=jnp.float32)
    projected = projected.reshape(query_count, col_count, narrow).transpose(1, 0, 2)
    own_out = jnp.sum(lax.all_to_all(projected, "col", 0, 0, tiled=True), axis=0)
    picked_shift = shifted[req_ids, my_picked]
    own_shift = lax.dynamic_slice_in_dim(
        picked_shift.reshape(query_count, full_width), first_feature, narrow, 1
    )
    hidden_out = (own_shift + own_out).astype(jnp.bfloat16).reshape(req_here, sel_count, narrow)
    return (joined_cache, hidden_out)


def solution(mesh):
    return jax.shard_map(
        per_device,
        mesh=mesh,
        in_specs=(
            P("row", None, None),
            P(),
            P(),
            P("row", "col"),
            P("row", None, "col"),
            P("col", "row"),
            P(),
            P(),
            P(),
        ),
        out_specs=(P("row", None, None, "col"), P("row", None, "col")),
        check_vma=False,
    )
```

```python
import jax
import jax.numpy as jnp
from jax import lax
from jax.sharding import PartitionSpec as P

HEADS = 25
HEAD_DIM = 64
REM_DEV = 32
ROW_RUN = 4
TOKEN_SPLIT = 4
HIGH = lax.Precision.HIGHEST


def layer_norm(shifted, ln_gain):
    center = shifted - jnp.mean(shifted, axis=-1, keepdims=True)
    spread = jnp.mean(center * center, axis=-1, keepdims=True)
    return center * lax.rsqrt(spread + 1e-05) * ln_gain.astype(jnp.float32)


def row_gather(block, row_count):
    run = ROW_RUN if row_count % ROW_RUN == 0 else 1
    runs = row_count // run
    inner = [block] + [
        lax.ppermute(block, "row", [(z * run + a, z * run + (a + s) % run) for z in range(runs) for a in range(run)])
        for s in range(1, run)
    ]
    stage = jnp.stack(inner)
    outer = [stage] + [
        lax.ppermute(stage, "row", [(z * run + a, ((z + s) % runs) * run + a) for z in range(runs) for a in range(run)])
        for s in range(1, runs)
    ]
    stacked = jnp.stack(outer)
    me = lax.axis_index("row")
    z, a = me // run, me % run
    src_z = (z - jnp.arange(runs)) % runs
    src_a = (a - jnp.arange(run)) % run
    order_z = jnp.argsort(src_z)
    order_a = jnp.argsort(src_a)
    ordered = stacked[order_z][:, order_a]
    return ordered.reshape((row_count,) + block.shape)


def gather_weights(w_query, w_keyval, w_out, row_count):
    q_rows, q_cols = w_query.shape
    o_rows, o_cols = w_out.shape
    pack = jnp.concatenate([w_query.reshape(-1), w_keyval.reshape(-1), w_out.reshape(-1)])
    allw = row_gather(pack, row_count)
    q_size = w_query.size
    kv_size = w_keyval.size
    query_rows = allw[:, :q_size].reshape(row_count * q_rows, q_cols)
    keyval_rows = allw[:, q_size:q_size + kv_size].reshape(row_count * q_rows, 2, q_cols)
    out_cols = (
        allw[:, q_size + kv_size:]
        .reshape(row_count, o_rows, o_cols)
        .transpose(1, 0, 2)
        .reshape(o_rows, row_count * o_cols)
    )
    return query_rows, keyval_rows, out_cols


def fetch_groups(group_store, group_src, row_count, row_index, col_count, col_index, req_here):
    slot_count, group_len, full_width = group_store.shape
    group_count = group_src.shape[1]
    ref_count = req_here * group_count
    local_count = ref_count - REM_DEV
    capacity = max(2, (REM_DEV + row_count - 2) // (row_count - 1))
    owner_src = group_src.reshape(row_count, ref_count)
    holder_all = owner_src // slot_count
    slot_all = owner_src % slot_count
    owner_ids = jnp.arange(row_count, dtype=jnp.int32)
    remote_all = holder_all != owner_ids[:, None]
    outgoing = remote_all & (holder_all == row_index)
    out_rank = jnp.cumsum(outgoing.astype(jnp.int32), axis=1) - 1
    slot_ids = jnp.arange(capacity, dtype=jnp.int32)
    chosen = outgoing[:, None, :] & (out_rank[:, None, :] == slot_ids[None, :, None])
    send_slot = jnp.sum(jnp.where(chosen, slot_all[:, None, :], 0), axis=2)
    send_live = jnp.any(chosen, axis=2)
    my_holder = lax.dynamic_index_in_dim(holder_all, row_index, 0, keepdims=False)
    my_slot = lax.dynamic_index_in_dim(slot_all, row_index, 0, keepdims=False)
    my_remote = lax.dynamic_index_in_dim(remote_all, row_index, 0, keepdims=False)
    incoming = (my_holder[None, :] == owner_ids[:, None]) & my_remote[None, :]
    in_rank = jnp.cumsum(incoming.astype(jnp.int32), axis=1) - 1
    my_rank = jnp.sum(jnp.where(incoming, in_rank, 0), axis=0)
    flat_index = my_holder * capacity + my_rank
    ordinal = jnp.cumsum(my_remote.astype(jnp.int32)) - 1
    compact_ids = jnp.arange(REM_DEV, dtype=jnp.int32)
    compact_pick = my_remote[None, :] & (ordinal[None, :] == compact_ids[:, None])
    compact_index = jnp.sum(jnp.where(compact_pick, flat_index[None, :], 0), axis=1)
    compact_ref = jnp.sum(jnp.where(compact_pick, jnp.arange(ref_count)[None, :], 0), axis=1)
    local_ordinal = jnp.cumsum((~my_remote).astype(jnp.int32)) - 1
    local_ids = jnp.arange(local_count, dtype=jnp.int32)
    local_pick = (~my_remote)[None, :] & (local_ordinal[None, :] == local_ids[:, None])
    local_ref = jnp.sum(jnp.where(local_pick, jnp.arange(ref_count)[None, :], 0), axis=1)
    local_slot = jnp.sum(jnp.where(local_pick, my_slot[None, :], 0), axis=1)

    split = TOKEN_SPLIT
    if col_count % split or group_len % split:
        split = 1
    part = group_len // split
    own_part = col_index % split
    store_rows = group_store.reshape(slot_count * group_len, full_width)
    tok_ids = jnp.arange(part, dtype=jnp.int32)
    send_rows = send_slot[:, :, None] * group_len + own_part * part + tok_ids
    payload = store_rows[send_rows.reshape(-1)].reshape(row_count, capacity * part, full_width)
    live_rows = jnp.repeat(send_live, part, axis=1)
    received = lax.all_to_all(
        jnp.where(live_rows[:, :, None], payload, jnp.zeros_like(payload)),
        "row",
        split_axis=0,
        concat_axis=0,
        tiled=True,
    )
    flat = received.reshape(row_count * capacity * part, full_width)
    compact = flat[(compact_index[:, None] * part + tok_ids).reshape(-1)]
    pieces = [compact] + [
        lax.ppermute(compact, "col", [(c, c ^ m) for c in range(col_count)]) for m in range(1, split)
    ]
    near_rows = (local_slot[:, None] * group_len + jnp.arange(group_len, dtype=jnp.int32)).reshape(-1)
    near = store_rows[near_rows]
    blocks = [near]
    refs = [jnp.repeat(local_ref, group_len)]
    toks = [jnp.tile(jnp.arange(group_len, dtype=jnp.int32), local_count)]
    for m in range(split):
        blocks.append(pieces[m])
        refs.append(jnp.repeat(compact_ref, part))
        toks.append(jnp.tile((own_part ^ m) * part + tok_ids, REM_DEV))
    ref_ids = jnp.arange(ref_count, dtype=jnp.int32)[:, None]
    tok_all = jnp.arange(group_len, dtype=jnp.int32)[None, :]
    remote_row = local_count * group_len + (
        ((tok_all // part) ^ own_part) * REM_DEV * part + ordinal[:, None] * part + tok_all % part
    )
    near_row = local_ordinal[:, None] * group_len + tok_all
    row_of = jnp.where(my_remote[:, None], remote_row, near_row)
    del ref_ids
    return blocks, refs, toks, row_of.reshape(-1)


def per_device(
    group_store, positions, ln_gain, w_query, w_keyval, w_out, group_src, lengths, selected
):
    row_count = lax.axis_size("row")
    col_count = lax.axis_size("col")
    row_index = lax.axis_index("row")
    col_index = lax.axis_index("col")
    slot_count, group_len, full_width = group_store.shape
    narrow = full_width // col_count
    req_here = lengths.shape[1]
    group_count = group_src.shape[1]
    token_span = group_count * group_len
    sel_count = selected.shape[1]
    query_count = req_here * sel_count
    first_feature = col_index * narrow

    query_rows, keyval_rows, out_cols = gather_weights(w_query, w_keyval, w_out, row_count)
    w_cat = jnp.concatenate([keyval_rows.reshape(full_width, 2 * narrow), query_rows], axis=1)
    blocks, refs, toks, row_of = fetch_groups(
        group_store, group_src, row_count, row_index, col_count, col_index, req_here
    )

    pos_f = positions.astype(jnp.float32)
    out_kv, out_q, out_sh = [], [], []
    for block, ref, tok in zip(blocks, refs, toks):
        place = (ref % group_count) * group_len + tok
        shifted = block.astype(jnp.float32) + pos_f[place] - pos_f[tok]
        normed = layer_norm(shifted, ln_gain).astype(jnp.bfloat16)
        both = jnp.dot(normed, w_cat, preferred_element_type=jnp.float32).astype(jnp.bfloat16)
        out_kv.append(both[:, : 2 * narrow])
        out_q.append(both[:, 2 * narrow:])
        out_sh.append(lax.dynamic_slice_in_dim(shifted, first_feature, narrow, 1))
    kv_rows = jnp.concatenate(out_kv)
    q_rows = jnp.concatenate(out_q)
    sh_rows = jnp.concatenate(out_sh)

    my_lengths = lax.dynamic_index_in_dim(lengths, row_index, 0, keepdims=False)
    my_picked = lax.dynamic_slice_in_dim(selected, row_index * req_here, req_here, 0)
    token_place = jnp.arange(token_span, dtype=jnp.int32)
    keyval = kv_rows[row_of].reshape(req_here, token_span, 2, narrow)
    alive = token_place[None, :] < (my_lengths * group_len)[:, None]
    joined_cache = jnp.where(alive[:, :, None, None], keyval, jnp.zeros_like(keyval))

    req_ids = jnp.arange(req_here, dtype=jnp.int32)[:, None]
    picked_row = row_of.reshape(req_here, token_span)[req_ids, my_picked]
    queries = q_rows[picked_row]
    picked_shift = sh_rows[picked_row]

    feature_head = (first_feature + jnp.arange(narrow, dtype=jnp.int32)) // HEAD_DIM
    first_head = first_feature // HEAD_DIM
    last_piece = (first_feature + narrow - 1) // HEAD_DIM - first_head
    piece_count = (narrow + 2 * HEAD_DIM - 2) // HEAD_DIM
    query_f = queries.astype(jnp.float32)
    key_f = joined_cache[:, :, 0].astype(jnp.float32)
    value_f = joined_cache[:, :, 1].astype(jnp.float32)
    masks = [feature_head == first_head + p for p in range(piece_count)]
    partial = [
        jnp.einsum(
            "bie,bte->bit", jnp.where(m[None, None, :], query_f, 0.0), key_f, precision=HIGH
        )
        for m in masks
    ]
    right_piece = partial[0]
    for p in range(1, piece_count):
        right_piece = jnp.where(last_piece == p, partial[p], right_piece)
    from_left = lax.ppermute(right_piece, "col", [(i, i + 1) for i in range(col_count - 1)])
    from_right = lax.ppermute(partial[0], "col", [(i + 1, i) for i in range(col_count - 1)])
    allowed = token_place[None, None, :] <= my_picked[:, :, None]
    attended = jnp.zeros((req_here, sel_count, narrow), jnp.float32)
    for p in range(piece_count):
        full = partial[p]
        if p == 0:
            full = full + from_left
        full = full + jnp.where(last_piece == p, from_right, 0.0)
        scores = jnp.where(allowed, full * 0.125, -1e30)
        highest = jnp.max(scores, axis=-1, keepdims=True)
        weights = jnp.where(allowed, jnp.exp(scores - highest), 0.0)
        totals = jnp.sum(weights, axis=-1)
        summed = jnp.einsum("bit,bte->bie", weights, value_f, precision=HIGH)
        attended = jnp.where(masks[p][None, None, :], summed / totals[:, :, None], attended)
    attended = attended.astype(jnp.bfloat16).reshape(query_count, narrow)

    projected = jnp.dot(attended, out_cols, preferred_element_type=jnp.float32)
    projected = projected.reshape(query_count, col_count, narrow).transpose(1, 0, 2)
    own_out = jnp.sum(lax.all_to_all(projected, "col", 0, 0, tiled=True), axis=0)
    hidden_out = (picked_shift.reshape(query_count, narrow) + own_out).astype(jnp.bfloat16)
    return (joined_cache, hidden_out.reshape(req_here, sel_count, narrow))


def solution(mesh):
    return jax.shard_map(
        per_device,
        mesh=mesh,
        in_specs=(
            P("row", None, None),
            P(),
            P(),
            P("row", "col"),
            P("row", None, "col"),
            P("col", "row"),
            P(),
            P(),
            P(),
        ),
        out_specs=(P("row", None, None, "col"), P("row", None, "col")),
        check_vma=False,
    )
```

```python
import jax
import jax.numpy as jnp
from jax import lax
from jax.sharding import PartitionSpec as P

HEADS = 25
HEAD_DIM = 64
REM_DEV = 32
TOKEN_SPLIT = 4
HIGH = lax.Precision.HIGHEST


def layer_norm(shifted, ln_gain):
    center = shifted - jnp.mean(shifted, axis=-1, keepdims=True)
    spread = jnp.mean(center * center, axis=-1, keepdims=True)
    return center * lax.rsqrt(spread + 1e-05) * ln_gain.astype(jnp.float32)


def split_weights(allw, w_query, w_keyval, w_out, row_count):
    q_rows, q_cols = w_query.shape
    o_rows, o_cols = w_out.shape
    q_size = w_query.size
    kv_size = w_keyval.size
    query_rows = allw[:, :q_size].reshape(row_count * q_rows, q_cols)
    keyval_rows = allw[:, q_size:q_size + kv_size].reshape(row_count * q_rows, 2, q_cols)
    out_cols = (
        allw[:, q_size + kv_size:]
        .reshape(row_count, o_rows, o_cols)
        .transpose(1, 0, 2)
        .reshape(o_rows, row_count * o_cols)
    )
    return query_rows, keyval_rows, out_cols


def fetch_groups(group_store, group_src, row_count, row_index, col_count, col_index, req_here, extra):
    slot_count, group_len, full_width = group_store.shape
    group_count = group_src.shape[1]
    ref_count = req_here * group_count
    local_count = ref_count - REM_DEV
    capacity = max(2, (REM_DEV + row_count - 2) // (row_count - 1))
    owner_src = group_src.reshape(row_count, ref_count)
    holder_all = owner_src // slot_count
    slot_all = owner_src % slot_count
    owner_ids = jnp.arange(row_count, dtype=jnp.int32)
    remote_all = holder_all != owner_ids[:, None]
    outgoing = remote_all & (holder_all == row_index)
    out_rank = jnp.cumsum(outgoing.astype(jnp.int32), axis=1) - 1
    slot_ids = jnp.arange(capacity, dtype=jnp.int32)
    chosen = outgoing[:, None, :] & (out_rank[:, None, :] == slot_ids[None, :, None])
    send_slot = jnp.sum(jnp.where(chosen, slot_all[:, None, :], 0), axis=2)
    send_live = jnp.any(chosen, axis=2)
    my_holder = lax.dynamic_index_in_dim(holder_all, row_index, 0, keepdims=False)
    my_slot = lax.dynamic_index_in_dim(slot_all, row_index, 0, keepdims=False)
    my_remote = lax.dynamic_index_in_dim(remote_all, row_index, 0, keepdims=False)
    incoming = (my_holder[None, :] == owner_ids[:, None]) & my_remote[None, :]
    in_rank = jnp.cumsum(incoming.astype(jnp.int32), axis=1) - 1
    my_rank = jnp.sum(jnp.where(incoming, in_rank, 0), axis=0)
    flat_index = my_holder * capacity + my_rank
    ordinal = jnp.cumsum(my_remote.astype(jnp.int32)) - 1
    compact_ids = jnp.arange(REM_DEV, dtype=jnp.int32)
    compact_pick = my_remote[None, :] & (ordinal[None, :] == compact_ids[:, None])
    compact_index = jnp.sum(jnp.where(compact_pick, flat_index[None, :], 0), axis=1)
    compact_ref = jnp.sum(jnp.where(compact_pick, jnp.arange(ref_count)[None, :], 0), axis=1)
    local_ordinal = jnp.cumsum((~my_remote).astype(jnp.int32)) - 1
    local_ids = jnp.arange(local_count, dtype=jnp.int32)
    local_pick = (~my_remote)[None, :] & (local_ordinal[None, :] == local_ids[:, None])
    local_ref = jnp.sum(jnp.where(local_pick, jnp.arange(ref_count)[None, :], 0), axis=1)
    local_slot = jnp.sum(jnp.where(local_pick, my_slot[None, :], 0), axis=1)

    split = TOKEN_SPLIT
    if col_count % split or group_len % split:
        split = 1
    part = group_len // split
    own_part = col_index % split
    store_rows = group_store.reshape(slot_count * group_len, full_width)
    tok_ids = jnp.arange(part, dtype=jnp.int32)
    send_rows = send_slot[:, :, None] * group_len + own_part * part + tok_ids
    payload = store_rows[send_rows.reshape(-1)].reshape(row_count, capacity * part, full_width)
    live_rows = jnp.repeat(send_live, part, axis=1)
    extra_rows = -(-extra.shape[0] // full_width)
    extra_pad = jnp.pad(extra, (0, extra_rows * full_width - extra.shape[0])).reshape(extra_rows, full_width)
    sent = jnp.concatenate(
        [
            jnp.where(live_rows[:, :, None], payload, jnp.zeros_like(payload)),
            jnp.broadcast_to(extra_pad[None], (row_count, extra_rows, full_width)),
        ],
        axis=1,
    )
    received = lax.all_to_all(sent, "row", split_axis=0, concat_axis=0, tiled=True)
    extra_all = received[:, capacity * part:].reshape(row_count, -1)[:, : extra.shape[0]]
    flat = received[:, : capacity * part].reshape(row_count * capacity * part, full_width)
    compact = flat[(compact_index[:, None] * part + tok_ids).reshape(-1)]
    pieces = [compact] + [
        lax.ppermute(compact, "col", [(c, c ^ m) for c in range(col_count)]) for m in range(1, split)
    ]
    near_rows = (local_slot[:, None] * group_len + jnp.arange(group_len, dtype=jnp.int32)).reshape(-1)
    near = store_rows[near_rows]
    blocks = [near]
    refs = [jnp.repeat(local_ref, group_len)]
    toks = [jnp.tile(jnp.arange(group_len, dtype=jnp.int32), local_count)]
    for m in range(split):
        blocks.append(pieces[m])
        refs.append(jnp.repeat(compact_ref, part))
        toks.append(jnp.tile((own_part ^ m) * part + tok_ids, REM_DEV))
    tok_all = jnp.arange(group_len, dtype=jnp.int32)[None, :]
    remote_row = local_count * group_len + (
        ((tok_all // part) ^ own_part) * REM_DEV * part + ordinal[:, None] * part + tok_all % part
    )
    near_row = local_ordinal[:, None] * group_len + tok_all
    row_of = jnp.where(my_remote[:, None], remote_row, near_row)
    return blocks, refs, toks, row_of.reshape(-1), extra_all


def per_device(
    group_store, positions, ln_gain, w_query, w_keyval, w_out, group_src, lengths, selected
):
    row_count = lax.axis_size("row")
    col_count = lax.axis_size("col")
    row_index = lax.axis_index("row")
    col_index = lax.axis_index("col")
    slot_count, group_len, full_width = group_store.shape
    narrow = full_width // col_count
    req_here = lengths.shape[1]
    group_count = group_src.shape[1]
    token_span = group_count * group_len
    sel_count = selected.shape[1]
    query_count = req_here * sel_count
    first_feature = col_index * narrow

    pack = jnp.concatenate([w_query.reshape(-1), w_keyval.reshape(-1), w_out.reshape(-1)])
    blocks, refs, toks, row_of, allw = fetch_groups(
        group_store, group_src, row_count, row_index, col_count, col_index, req_here, pack
    )
    query_rows, keyval_rows, out_cols = split_weights(allw, w_query, w_keyval, w_out, row_count)
    w_cat = jnp.concatenate([keyval_rows.reshape(full_width, 2 * narrow), query_rows], axis=1)

    pos_f = positions.astype(jnp.float32)
    out_kv, out_q, out_sh = [], [], []
    for block, ref, tok in zip(blocks, refs, toks):
        place = (ref % group_count) * group_len + tok
        shifted = block.astype(jnp.float32) + pos_f[place] - pos_f[tok]
        normed = layer_norm(shifted, ln_gain).astype(jnp.bfloat16)
        both = jnp.dot(normed, w_cat, preferred_element_type=jnp.float32).astype(jnp.bfloat16)
        out_kv.append(both[:, : 2 * narrow])
        out_q.append(both[:, 2 * narrow:])
        out_sh.append(lax.dynamic_slice_in_dim(shifted, first_feature, narrow, 1))
    kv_rows = jnp.concatenate(out_kv)
    q_rows = jnp.concatenate(out_q)
    sh_rows = jnp.concatenate(out_sh)

    my_lengths = lax.dynamic_index_in_dim(lengths, row_index, 0, keepdims=False)
    my_picked = lax.dynamic_slice_in_dim(selected, row_index * req_here, req_here, 0)
    token_place = jnp.arange(token_span, dtype=jnp.int32)
    keyval = kv_rows[row_of].reshape(req_here, token_span, 2, narrow)
    alive = token_place[None, :] < (my_lengths * group_len)[:, None]
    joined_cache = jnp.where(alive[:, :, None, None], keyval, jnp.zeros_like(keyval))

    req_ids = jnp.arange(req_here, dtype=jnp.int32)[:, None]
    picked_row = row_of.reshape(req_here, token_span)[req_ids, my_picked]
    queries = q_rows[picked_row]
    picked_shift = sh_rows[picked_row]

    feature_head = (first_feature + jnp.arange(narrow, dtype=jnp.int32)) // HEAD_DIM
    first_head = first_feature // HEAD_DIM
    last_piece = (first_feature + narrow - 1) // HEAD_DIM - first_head
    piece_count = (narrow + 2 * HEAD_DIM - 2) // HEAD_DIM
    query_f = queries.astype(jnp.float32)
    key_f = joined_cache[:, :, 0].astype(jnp.float32)
    value_f = joined_cache[:, :, 1].astype(jnp.float32)
    masks = [feature_head == first_head + p for p in range(piece_count)]
    partial = [
        jnp.einsum(
            "bie,bte->bit", jnp.where(m[None, None, :], query_f, 0.0), key_f, precision=HIGH
        )
        for m in masks
    ]
    right_piece = partial[0]
    for p in range(1, piece_count):
        right_piece = jnp.where(last_piece == p, partial[p], right_piece)
    from_left = lax.ppermute(right_piece, "col", [(i, i + 1) for i in range(col_count - 1)])
    from_right = lax.ppermute(partial[0], "col", [(i + 1, i) for i in range(col_count - 1)])
    allowed = token_place[None, None, :] <= my_picked[:, :, None]
    attended = jnp.zeros((req_here, sel_count, narrow), jnp.float32)
    for p in range(piece_count):
        full = partial[p]
        if p == 0:
            full = full + from_left
        full = full + jnp.where(last_piece == p, from_right, 0.0)
        scores = jnp.where(allowed, full * 0.125, -1e30)
        highest = jnp.max(scores, axis=-1, keepdims=True)
        weights = jnp.where(allowed, jnp.exp(scores - highest), 0.0)
        totals = jnp.sum(weights, axis=-1)
        summed = jnp.einsum("bit,bte->bie", weights, value_f, precision=HIGH)
        attended = jnp.where(masks[p][None, None, :], summed / totals[:, :, None], attended)
    attended = attended.astype(jnp.bfloat16).reshape(query_count, narrow)

    projected = jnp.dot(attended, out_cols, preferred_element_type=jnp.float32)
    projected = projected.reshape(query_count, col_count, narrow).transpose(1, 0, 2)
    own_out = jnp.sum(lax.all_to_all(projected, "col", 0, 0, tiled=True), axis=0)
    hidden_out = (picked_shift.reshape(query_count, narrow) + own_out).astype(jnp.bfloat16)
    return (joined_cache, hidden_out.reshape(req_here, sel_count, narrow))


def solution(mesh):
    return jax.shard_map(
        per_device,
        mesh=mesh,
        in_specs=(
            P("row", None, None),
            P(),
            P(),
            P("row", "col"),
            P("row", None, "col"),
            P("col", "row"),
            P(),
            P(),
            P(),
        ),
        out_specs=(P("row", None, None, "col"), P("row", None, "col")),
        check_vma=False,
    )
```

```python
import jax
import jax.numpy as jnp
from jax import lax
from jax.sharding import PartitionSpec as P

HEADS = 25
HEAD_DIM = 64
REM_DEV = 32
TOKEN_SPLIT = 4
HIGH = lax.Precision.HIGHEST


def layer_norm(shifted, ln_gain):
    center = shifted - jnp.mean(shifted, axis=-1, keepdims=True)
    spread = jnp.mean(center * center, axis=-1, keepdims=True)
    return center * lax.rsqrt(spread + 1e-05) * ln_gain.astype(jnp.float32)


def split_weights(allw, w_query, w_keyval, w_out, row_count):
    q_rows, q_cols = w_query.shape
    o_rows, o_cols = w_out.shape
    q_size = w_query.size
    kv_size = w_keyval.size
    query_rows = allw[:, :q_size].reshape(row_count * q_rows, q_cols)
    keyval_rows = allw[:, q_size:q_size + kv_size].reshape(row_count * q_rows, 2, q_cols)
    out_cols = (
        allw[:, q_size + kv_size:]
        .reshape(row_count, o_rows, o_cols)
        .transpose(1, 0, 2)
        .reshape(o_rows, row_count * o_cols)
    )
    return query_rows, keyval_rows, out_cols


def fetch_groups(group_store, group_src, row_count, row_index, col_count, col_index, req_here, extra):
    slot_count, group_len, full_width = group_store.shape
    group_count = group_src.shape[1]
    ref_count = req_here * group_count
    local_count = ref_count - REM_DEV
    capacity = max(2, (REM_DEV + row_count - 2) // (row_count - 1))
    owner_src = group_src.reshape(row_count, ref_count)
    holder_all = owner_src // slot_count
    slot_all = owner_src % slot_count
    owner_ids = jnp.arange(row_count, dtype=jnp.int32)
    remote_all = holder_all != owner_ids[:, None]
    outgoing = remote_all & (holder_all == row_index)
    out_rank = jnp.cumsum(outgoing.astype(jnp.int32), axis=1) - 1
    slot_ids = jnp.arange(capacity, dtype=jnp.int32)
    chosen = outgoing[:, None, :] & (out_rank[:, None, :] == slot_ids[None, :, None])
    send_slot = jnp.sum(jnp.where(chosen, slot_all[:, None, :], 0), axis=2)
    send_live = jnp.any(chosen, axis=2)
    my_holder = lax.dynamic_index_in_dim(holder_all, row_index, 0, keepdims=False)
    my_slot = lax.dynamic_index_in_dim(slot_all, row_index, 0, keepdims=False)
    my_remote = lax.dynamic_index_in_dim(remote_all, row_index, 0, keepdims=False)
    incoming = (my_holder[None, :] == owner_ids[:, None]) & my_remote[None, :]
    in_rank = jnp.cumsum(incoming.astype(jnp.int32), axis=1) - 1
    my_rank = jnp.sum(jnp.where(incoming, in_rank, 0), axis=0)
    flat_index = my_holder * capacity + my_rank
    ordinal = jnp.cumsum(my_remote.astype(jnp.int32)) - 1
    compact_ids = jnp.arange(REM_DEV, dtype=jnp.int32)
    compact_pick = my_remote[None, :] & (ordinal[None, :] == compact_ids[:, None])
    compact_index = jnp.sum(jnp.where(compact_pick, flat_index[None, :], 0), axis=1)
    compact_ref = jnp.sum(jnp.where(compact_pick, jnp.arange(ref_count)[None, :], 0), axis=1)
    local_ordinal = jnp.cumsum((~my_remote).astype(jnp.int32)) - 1
    local_ids = jnp.arange(local_count, dtype=jnp.int32)
    local_pick = (~my_remote)[None, :] & (local_ordinal[None, :] == local_ids[:, None])
    local_ref = jnp.sum(jnp.where(local_pick, jnp.arange(ref_count)[None, :], 0), axis=1)
    local_slot = jnp.sum(jnp.where(local_pick, my_slot[None, :], 0), axis=1)

    split = TOKEN_SPLIT
    if col_count % split or group_len % split:
        split = 1
    part = group_len // split
    own_part = col_index % split
    store_rows = group_store.reshape(slot_count * group_len, full_width)
    tok_ids = jnp.arange(part, dtype=jnp.int32)
    send_rows = send_slot[:, :, None] * group_len + own_part * part + tok_ids
    payload = store_rows[send_rows.reshape(-1)].reshape(row_count, capacity * part, full_width)
    live_rows = jnp.repeat(send_live, part, axis=1)
    sent = jnp.where(live_rows[:, :, None], payload, jnp.zeros_like(payload))
    received = lax.all_to_all(sent, "row", split_axis=0, concat_axis=0, tiled=True)
    extra, received = lax.optimization_barrier((extra, received))
    extra_all = lax.all_to_all(
        jnp.broadcast_to(extra[None], (row_count,) + extra.shape), "row", 0, 0, tiled=True
    )
    flat = received.reshape(row_count * capacity * part, full_width)
    compact = flat[(compact_index[:, None] * part + tok_ids).reshape(-1)]
    pieces = [compact] + [
        lax.ppermute(compact, "col", [(c, c ^ m) for c in range(col_count)]) for m in range(1, split)
    ]
    near_rows = (local_slot[:, None] * group_len + jnp.arange(group_len, dtype=jnp.int32)).reshape(-1)
    near = store_rows[near_rows]
    blocks = [near]
    refs = [jnp.repeat(local_ref, group_len)]
    toks = [jnp.tile(jnp.arange(group_len, dtype=jnp.int32), local_count)]
    for m in range(split):
        blocks.append(pieces[m])
        refs.append(jnp.repeat(compact_ref, part))
        toks.append(jnp.tile((own_part ^ m) * part + tok_ids, REM_DEV))
    tok_all = jnp.arange(group_len, dtype=jnp.int32)[None, :]
    remote_row = local_count * group_len + (
        ((tok_all // part) ^ own_part) * REM_DEV * part + ordinal[:, None] * part + tok_all % part
    )
    near_row = local_ordinal[:, None] * group_len + tok_all
    row_of = jnp.where(my_remote[:, None], remote_row, near_row)
    return blocks, refs, toks, row_of.reshape(-1), extra_all


def per_device(
    group_store, positions, ln_gain, w_query, w_keyval, w_out, group_src, lengths, selected
):
    row_count = lax.axis_size("row")
    col_count = lax.axis_size("col")
    row_index = lax.axis_index("row")
    col_index = lax.axis_index("col")
    slot_count, group_len, full_width = group_store.shape
    narrow = full_width // col_count
    req_here = lengths.shape[1]
    group_count = group_src.shape[1]
    token_span = group_count * group_len
    sel_count = selected.shape[1]
    query_count = req_here * sel_count
    first_feature = col_index * narrow

    pack = jnp.concatenate([w_query.reshape(-1), w_keyval.reshape(-1), w_out.reshape(-1)])
    blocks, refs, toks, row_of, allw = fetch_groups(
        group_store, group_src, row_count, row_index, col_count, col_index, req_here, pack
    )
    query_rows, keyval_rows, out_cols = split_weights(allw, w_query, w_keyval, w_out, row_count)
    w_cat = jnp.concatenate([keyval_rows.reshape(full_width, 2 * narrow), query_rows], axis=1)

    pos_f = positions.astype(jnp.float32)
    out_kv, out_q, out_sh = [], [], []
    for block, ref, tok in zip(blocks, refs, toks):
        place = (ref % group_count) * group_len + tok
        shifted = block.astype(jnp.float32) + pos_f[place] - pos_f[tok]
        normed = layer_norm(shifted, ln_gain).astype(jnp.bfloat16)
        both = jnp.dot(normed, w_cat, preferred_element_type=jnp.float32).astype(jnp.bfloat16)
        out_kv.append(both[:, : 2 * narrow])
        out_q.append(both[:, 2 * narrow:])
        out_sh.append(lax.dynamic_slice_in_dim(shifted, first_feature, narrow, 1))
    kv_rows = jnp.concatenate(out_kv)
    q_rows = jnp.concatenate(out_q)
    sh_rows = jnp.concatenate(out_sh)

    my_lengths = lax.dynamic_index_in_dim(lengths, row_index, 0, keepdims=False)
    my_picked = lax.dynamic_slice_in_dim(selected, row_index * req_here, req_here, 0)
    token_place = jnp.arange(token_span, dtype=jnp.int32)
    keyval = kv_rows[row_of].reshape(req_here, token_span, 2, narrow)
    alive = token_place[None, :] < (my_lengths * group_len)[:, None]
    joined_cache = jnp.where(alive[:, :, None, None], keyval, jnp.zeros_like(keyval))

    req_ids = jnp.arange(req_here, dtype=jnp.int32)[:, None]
    picked_row = row_of.reshape(req_here, token_span)[req_ids, my_picked]
    queries = q_rows[picked_row]
    picked_shift = sh_rows[picked_row]

    feature_head = (first_feature + jnp.arange(narrow, dtype=jnp.int32)) // HEAD_DIM
    first_head = first_feature // HEAD_DIM
    last_piece = (first_feature + narrow - 1) // HEAD_DIM - first_head
    piece_count = (narrow + 2 * HEAD_DIM - 2) // HEAD_DIM
    query_f = queries.astype(jnp.float32)
    key_f = joined_cache[:, :, 0].astype(jnp.float32)
    value_f = joined_cache[:, :, 1].astype(jnp.float32)
    masks = [feature_head == first_head + p for p in range(piece_count)]
    partial = [
        jnp.einsum(
            "bie,bte->bit", jnp.where(m[None, None, :], query_f, 0.0), key_f, precision=HIGH
        )
        for m in masks
    ]
    right_piece = partial[0]
    for p in range(1, piece_count):
        right_piece = jnp.where(last_piece == p, partial[p], right_piece)
    from_left = lax.ppermute(right_piece, "col", [(i, i + 1) for i in range(col_count - 1)])
    from_right = lax.ppermute(partial[0], "col", [(i + 1, i) for i in range(col_count - 1)])
    allowed = token_place[None, None, :] <= my_picked[:, :, None]
    attended = jnp.zeros((req_here, sel_count, narrow), jnp.float32)
    for p in range(piece_count):
        full = partial[p]
        if p == 0:
            full = full + from_left
        full = full + jnp.where(last_piece == p, from_right, 0.0)
        scores = jnp.where(allowed, full * 0.125, -1e30)
        highest = jnp.max(scores, axis=-1, keepdims=True)
        weights = jnp.where(allowed, jnp.exp(scores - highest), 0.0)
        totals = jnp.sum(weights, axis=-1)
        summed = jnp.einsum("bit,bte->bie", weights, value_f, precision=HIGH)
        attended = jnp.where(masks[p][None, None, :], summed / totals[:, :, None], attended)
    attended = attended.astype(jnp.bfloat16).reshape(query_count, narrow)

    projected = jnp.dot(attended, out_cols, preferred_element_type=jnp.float32)
    projected = projected.reshape(query_count, col_count, narrow).transpose(1, 0, 2)
    own_out = jnp.sum(lax.all_to_all(projected, "col", 0, 0, tiled=True), axis=0)
    hidden_out = (picked_shift.reshape(query_count, narrow) + own_out).astype(jnp.bfloat16)
    return (joined_cache, hidden_out.reshape(req_here, sel_count, narrow))


def solution(mesh):
    return jax.shard_map(
        per_device,
        mesh=mesh,
        in_specs=(
            P("row", None, None),
            P(),
            P(),
            P("row", "col"),
            P("row", None, "col"),
            P("col", "row"),
            P(),
            P(),
            P(),
        ),
        out_specs=(P("row", None, None, "col"), P("row", None, "col")),
        check_vma=False,
    )
```

```python
import jax
import jax.numpy as jnp
from jax import lax
from jax.sharding import PartitionSpec as P

HEADS = 25
HEAD_DIM = 64
REM_DEV = 32
TOKEN_SPLIT = 4
HIGH = lax.Precision.HIGHEST


def layer_norm(shifted, ln_gain):
    center = shifted - jnp.mean(shifted, axis=-1, keepdims=True)
    spread = jnp.mean(center * center, axis=-1, keepdims=True)
    return center * lax.rsqrt(spread + 1e-05) * ln_gain.astype(jnp.float32)


def fetch_groups(group_store, group_src, row_count, row_index, col_count, col_index, req_here, extra):
    slot_count, group_len, full_width = group_store.shape
    group_count = group_src.shape[1]
    ref_count = req_here * group_count
    local_count = ref_count - REM_DEV
    capacity = max(2, (REM_DEV + row_count - 2) // (row_count - 1))
    owner_src = group_src.reshape(row_count, ref_count)
    holder_all = owner_src // slot_count
    slot_all = owner_src % slot_count
    owner_ids = jnp.arange(row_count, dtype=jnp.int32)
    remote_all = holder_all != owner_ids[:, None]
    outgoing = remote_all & (holder_all == row_index)
    out_rank = jnp.cumsum(outgoing.astype(jnp.int32), axis=1) - 1
    slot_ids = jnp.arange(capacity, dtype=jnp.int32)
    chosen = outgoing[:, None, :] & (out_rank[:, None, :] == slot_ids[None, :, None])
    send_slot = jnp.sum(jnp.where(chosen, slot_all[:, None, :], 0), axis=2)
    send_live = jnp.any(chosen, axis=2)
    my_holder = lax.dynamic_index_in_dim(holder_all, row_index, 0, keepdims=False)
    my_slot = lax.dynamic_index_in_dim(slot_all, row_index, 0, keepdims=False)
    my_remote = lax.dynamic_index_in_dim(remote_all, row_index, 0, keepdims=False)
    incoming = (my_holder[None, :] == owner_ids[:, None]) & my_remote[None, :]
    in_rank = jnp.cumsum(incoming.astype(jnp.int32), axis=1) - 1
    my_rank = jnp.sum(jnp.where(incoming, in_rank, 0), axis=0)
    flat_index = my_holder * capacity + my_rank
    ordinal = jnp.cumsum(my_remote.astype(jnp.int32)) - 1
    compact_ids = jnp.arange(REM_DEV, dtype=jnp.int32)
    compact_pick = my_remote[None, :] & (ordinal[None, :] == compact_ids[:, None])
    compact_index = jnp.sum(jnp.where(compact_pick, flat_index[None, :], 0), axis=1)
    compact_ref = jnp.sum(jnp.where(compact_pick, jnp.arange(ref_count)[None, :], 0), axis=1)
    local_ordinal = jnp.cumsum((~my_remote).astype(jnp.int32)) - 1
    local_ids = jnp.arange(local_count, dtype=jnp.int32)
    local_pick = (~my_remote)[None, :] & (local_ordinal[None, :] == local_ids[:, None])
    local_ref = jnp.sum(jnp.where(local_pick, jnp.arange(ref_count)[None, :], 0), axis=1)
    local_slot = jnp.sum(jnp.where(local_pick, my_slot[None, :], 0), axis=1)

    split = TOKEN_SPLIT
    if col_count % split or group_len % split:
        split = 1
    part = group_len // split
    own_part = col_index % split
    store_rows = group_store.reshape(slot_count * group_len, full_width)
    tok_ids = jnp.arange(part, dtype=jnp.int32)
    send_rows = send_slot[:, :, None] * group_len + own_part * part + tok_ids
    payload = store_rows[send_rows.reshape(-1)].reshape(row_count, capacity * part, full_width)
    live_rows = jnp.repeat(send_live, part, axis=1)
    sent = jnp.where(live_rows[:, :, None], payload, jnp.zeros_like(payload))
    received = lax.all_to_all(sent, "row", split_axis=0, concat_axis=0, tiled=True)
    extra, received = lax.optimization_barrier((extra, received))
    extra_all = lax.all_to_all(
        jnp.broadcast_to(extra[None], (row_count,) + extra.shape), "row", 0, 0, tiled=True
    )
    flat = received.reshape(row_count * capacity * part, full_width)
    compact = flat[(compact_index[:, None] * part + tok_ids).reshape(-1)]
    pieces = [compact] + [
        lax.ppermute(compact, "col", [(c, c ^ m) for c in range(col_count)]) for m in range(1, split)
    ]
    near_rows = (local_slot[:, None] * group_len + jnp.arange(group_len, dtype=jnp.int32)).reshape(-1)
    near = store_rows[near_rows]
    blocks = [near]
    refs = [jnp.repeat(local_ref, group_len)]
    toks = [jnp.tile(jnp.arange(group_len, dtype=jnp.int32), local_count)]
    for m in range(split):
        blocks.append(pieces[m])
        refs.append(jnp.repeat(compact_ref, part))
        toks.append(jnp.tile((own_part ^ m) * part + tok_ids, REM_DEV))
    tok_all = jnp.arange(group_len, dtype=jnp.int32)[None, :]
    remote_row = local_count * group_len + (
        ((tok_all // part) ^ own_part) * REM_DEV * part + ordinal[:, None] * part + tok_all % part
    )
    near_row = local_ordinal[:, None] * group_len + tok_all
    row_of = jnp.where(my_remote[:, None], remote_row, near_row)
    return blocks, refs, toks, row_of.reshape(-1), extra_all


def per_device(
    group_store, positions, ln_gain, w_query, w_keyval, w_out, group_src, lengths, selected
):
    row_count = lax.axis_size("row")
    col_count = lax.axis_size("col")
    row_index = lax.axis_index("row")
    col_index = lax.axis_index("col")
    slot_count, group_len, full_width = group_store.shape
    narrow = full_width // col_count
    req_here = lengths.shape[1]
    group_count = group_src.shape[1]
    token_span = group_count * group_len
    sel_count = selected.shape[1]
    query_count = req_here * sel_count
    first_feature = col_index * narrow

    pack = jnp.concatenate(
        [w_keyval.reshape(w_keyval.shape[0], 2 * narrow), w_query, w_out.T], axis=1
    )
    blocks, refs, toks, row_of, allw = fetch_groups(
        group_store, group_src, row_count, row_index, col_count, col_index, req_here, pack
    )
    allw = allw.reshape(full_width, 4 * narrow)
    w_cat = allw[:, : 3 * narrow]
    out_rows = allw[:, 3 * narrow:]

    pos_f = positions.astype(jnp.float32)
    out_kv, out_q, out_sh = [], [], []
    for block, ref, tok in zip(blocks, refs, toks):
        place = (ref % group_count) * group_len + tok
        shifted = block.astype(jnp.float32) + pos_f[place] - pos_f[tok]
        normed = layer_norm(shifted, ln_gain).astype(jnp.bfloat16)
        both = jnp.dot(normed, w_cat, preferred_element_type=jnp.float32).astype(jnp.bfloat16)
        out_kv.append(both[:, : 2 * narrow])
        out_q.append(both[:, 2 * narrow:])
        out_sh.append(lax.dynamic_slice_in_dim(shifted, first_feature, narrow, 1))
    kv_rows = jnp.concatenate(out_kv)
    q_rows = jnp.concatenate(out_q)
    sh_rows = jnp.concatenate(out_sh)

    my_lengths = lax.dynamic_index_in_dim(lengths, row_index, 0, keepdims=False)
    my_picked = lax.dynamic_slice_in_dim(selected, row_index * req_here, req_here, 0)
    token_place = jnp.arange(token_span, dtype=jnp.int32)
    keyval = kv_rows[row_of].reshape(req_here, token_span, 2, narrow)
    alive = token_place[None, :] < (my_lengths * group_len)[:, None]
    joined_cache = jnp.where(alive[:, :, None, None], keyval, jnp.zeros_like(keyval))

    req_ids = jnp.arange(req_here, dtype=jnp.int32)[:, None]
    picked_row = row_of.reshape(req_here, token_span)[req_ids, my_picked]
    queries = q_rows[picked_row]
    picked_shift = sh_rows[picked_row]

    feature_head = (first_feature + jnp.arange(narrow, dtype=jnp.int32)) // HEAD_DIM
    first_head = first_feature // HEAD_DIM
    last_piece = (first_feature + narrow - 1) // HEAD_DIM - first_head
    piece_count = (narrow + 2 * HEAD_DIM - 2) // HEAD_DIM
    query_f = queries.astype(jnp.float32)
    key_f = joined_cache[:, :, 0].astype(jnp.float32)
    value_f = joined_cache[:, :, 1].astype(jnp.float32)
    masks = [feature_head == first_head + p for p in range(piece_count)]
    partial = [
        jnp.einsum(
            "bie,bte->bit", jnp.where(m[None, None, :], query_f, 0.0), key_f, precision=HIGH
        )
        for m in masks
    ]
    right_piece = partial[0]
    for p in range(1, piece_count):
        right_piece = jnp.where(last_piece == p, partial[p], right_piece)
    from_left = lax.ppermute(right_piece, "col", [(i, i + 1) for i in range(col_count - 1)])
    from_right = lax.ppermute(partial[0], "col", [(i + 1, i) for i in range(col_count - 1)])
    allowed = token_place[None, None, :] <= my_picked[:, :, None]
    attended = jnp.zeros((req_here, sel_count, narrow), jnp.float32)
    for p in range(piece_count):
        full = partial[p]
        if p == 0:
            full = full + from_left
        full = full + jnp.where(last_piece == p, from_right, 0.0)
        scores = jnp.where(allowed, full * 0.125, -1e30)
        highest = jnp.max(scores, axis=-1, keepdims=True)
        weights = jnp.where(allowed, jnp.exp(scores - highest), 0.0)
        totals = jnp.sum(weights, axis=-1)
        summed = jnp.einsum("bit,bte->bie", weights, value_f, precision=HIGH)
        attended = jnp.where(masks[p][None, None, :], summed / totals[:, :, None], attended)
    attended = attended.astype(jnp.bfloat16).reshape(query_count, narrow)

    projected = lax.dot_general(
        attended, out_rows, (((1,), (1,)), ((), ())), preferred_element_type=jnp.float32
    )
    projected = projected.reshape(query_count, col_count, narrow).transpose(1, 0, 2)
    own_out = jnp.sum(lax.all_to_all(projected, "col", 0, 0, tiled=True), axis=0)
    hidden_out = (picked_shift.reshape(query_count, narrow) + own_out).astype(jnp.bfloat16)
    return (joined_cache, hidden_out.reshape(req_here, sel_count, narrow))


def solution(mesh):
    return jax.shard_map(
        per_device,
        mesh=mesh,
        in_specs=(
            P("row", None, None),
            P(),
            P(),
            P("row", "col"),
            P("row", None, "col"),
            P("col", "row"),
            P(),
            P(),
            P(),
        ),
        out_specs=(P("row", None, None, "col"), P("row", None, "col")),
        check_vma=False,
    )
```

```python
import jax
import jax.numpy as jnp
from jax import lax
from jax.sharding import PartitionSpec as P

HEADS = 25
HEAD_DIM = 64
REM_DEV = 32
TOKEN_SPLIT = 4
HIGH = lax.Precision.HIGHEST


def layer_norm(shifted, ln_gain):
    center = shifted - jnp.mean(shifted, axis=-1, keepdims=True)
    spread = jnp.mean(center * center, axis=-1, keepdims=True)
    return center * lax.rsqrt(spread + 1e-05) * ln_gain.astype(jnp.float32)


def fetch_groups(group_store, group_src, row_count, row_index, col_count, col_index, req_here, extra):
    slot_count, group_len, full_width = group_store.shape
    group_count = group_src.shape[1]
    ref_count = req_here * group_count
    local_count = ref_count - REM_DEV
    capacity = max(2, (REM_DEV + row_count - 2) // (row_count - 1))
    owner_src = group_src.reshape(row_count, ref_count)
    holder_all = owner_src // slot_count
    slot_all = owner_src % slot_count
    owner_ids = jnp.arange(row_count, dtype=jnp.int32)
    remote_all = holder_all != owner_ids[:, None]
    outgoing = remote_all & (holder_all == row_index)
    out_rank = jnp.cumsum(outgoing.astype(jnp.int32), axis=1) - 1
    slot_ids = jnp.arange(capacity, dtype=jnp.int32)
    chosen = outgoing[:, None, :] & (out_rank[:, None, :] == slot_ids[None, :, None])
    send_slot = jnp.sum(jnp.where(chosen, slot_all[:, None, :], 0), axis=2)
    send_live = jnp.any(chosen, axis=2)
    my_holder = lax.dynamic_index_in_dim(holder_all, row_index, 0, keepdims=False)
    my_slot = lax.dynamic_index_in_dim(slot_all, row_index, 0, keepdims=False)
    my_remote = lax.dynamic_index_in_dim(remote_all, row_index, 0, keepdims=False)
    incoming = (my_holder[None, :] == owner_ids[:, None]) & my_remote[None, :]
    in_rank = jnp.cumsum(incoming.astype(jnp.int32), axis=1) - 1
    my_rank = jnp.sum(jnp.where(incoming, in_rank, 0), axis=0)
    flat_index = my_holder * capacity + my_rank
    ordinal = jnp.cumsum(my_remote.astype(jnp.int32)) - 1
    compact_ids = jnp.arange(REM_DEV, dtype=jnp.int32)
    compact_pick = my_remote[None, :] & (ordinal[None, :] == compact_ids[:, None])
    compact_index = jnp.sum(jnp.where(compact_pick, flat_index[None, :], 0), axis=1)
    compact_ref = jnp.sum(jnp.where(compact_pick, jnp.arange(ref_count)[None, :], 0), axis=1)
    local_ordinal = jnp.cumsum((~my_remote).astype(jnp.int32)) - 1
    local_ids = jnp.arange(local_count, dtype=jnp.int32)
    local_pick = (~my_remote)[None, :] & (local_ordinal[None, :] == local_ids[:, None])
    local_ref = jnp.sum(jnp.where(local_pick, jnp.arange(ref_count)[None, :], 0), axis=1)
    local_slot = jnp.sum(jnp.where(local_pick, my_slot[None, :], 0), axis=1)

    split = TOKEN_SPLIT
    if col_count % split or group_len % split:
        split = 1
    part = group_len // split
    own_part = col_index % split
    store_rows = group_store.reshape(slot_count * group_len, full_width)
    tok_ids = jnp.arange(part, dtype=jnp.int32)
    send_rows = send_slot[:, :, None] * group_len + own_part * part + tok_ids
    payload = store_rows[send_rows.reshape(-1)].reshape(row_count, capacity * part, full_width)
    live_rows = jnp.repeat(send_live, part, axis=1)
    sent = jnp.where(live_rows[:, :, None], payload, jnp.zeros_like(payload))
    received = lax.all_to_all(sent, "row", split_axis=0, concat_axis=0, tiled=True)
    extra, received = lax.optimization_barrier((extra, received))
    extra_all = lax.all_to_all(
        jnp.broadcast_to(extra[None], (row_count,) + extra.shape), "row", 0, 0, tiled=True
    )
    flat = received.reshape(row_count * capacity * part, full_width)
    compact = flat[(compact_index[:, None] * part + tok_ids).reshape(-1)]
    pieces = [compact] + [
        lax.ppermute(compact, "col", [(c, c ^ m) for c in range(col_count)]) for m in range(1, split)
    ]
    near_rows = (local_slot[:, None] * group_len + jnp.arange(group_len, dtype=jnp.int32)).reshape(-1)
    near = store_rows[near_rows]
    blocks = [near]
    refs = [jnp.repeat(local_ref, group_len)]
    toks = [(0, group_len)]
    for m in range(split):
        blocks.append(pieces[m])
        refs.append(jnp.repeat(compact_ref, part))
        toks.append(((own_part ^ m) * part, part))
    tok_all = jnp.arange(group_len, dtype=jnp.int32)[None, :]
    remote_row = local_count * group_len + (
        ((tok_all // part) ^ own_part) * REM_DEV * part + ordinal[:, None] * part + tok_all % part
    )
    near_row = local_ordinal[:, None] * group_len + tok_all
    row_of = jnp.where(my_remote[:, None], remote_row, near_row)
    return blocks, refs, toks, row_of.reshape(-1), extra_all


def per_device(
    group_store, positions, ln_gain, w_query, w_keyval, w_out, group_src, lengths, selected
):
    row_count = lax.axis_size("row")
    col_count = lax.axis_size("col")
    row_index = lax.axis_index("row")
    col_index = lax.axis_index("col")
    slot_count, group_len, full_width = group_store.shape
    narrow = full_width // col_count
    req_here = lengths.shape[1]
    group_count = group_src.shape[1]
    token_span = group_count * group_len
    sel_count = selected.shape[1]
    query_count = req_here * sel_count
    first_feature = col_index * narrow

    pack = jnp.concatenate(
        [w_keyval.reshape(w_keyval.shape[0], 2 * narrow), w_query, w_out.T], axis=1
    )
    blocks, refs, toks, row_of, allw = fetch_groups(
        group_store, group_src, row_count, row_index, col_count, col_index, req_here, pack
    )
    allw = allw.reshape(full_width, 4 * narrow)
    w_cat = allw[:, : 3 * narrow]
    out_rows = allw[:, 3 * narrow:]

    out_kv, out_q, out_sh = [], [], []
    for block, ref, (tok_start, tok_len) in zip(blocks, refs, toks):
        groups_in = block.shape[0] // tok_len
        tok = tok_start + jnp.tile(jnp.arange(tok_len, dtype=jnp.int32), groups_in)
        place = (ref % group_count) * group_len + tok
        pos_place = positions[place].astype(jnp.float32)
        pos_tok = lax.dynamic_slice_in_dim(positions, tok_start, tok_len, 0).astype(jnp.float32)
        pos_tok = jnp.broadcast_to(pos_tok[None], (groups_in, tok_len, full_width)).reshape(block.shape)
        shifted = block.astype(jnp.float32) + pos_place - pos_tok
        normed = layer_norm(shifted, ln_gain).astype(jnp.bfloat16)
        both = jnp.dot(normed, w_cat, preferred_element_type=jnp.float32).astype(jnp.bfloat16)
        out_kv.append(both[:, : 2 * narrow])
        out_q.append(both[:, 2 * narrow:])
        out_sh.append(lax.dynamic_slice_in_dim(shifted, first_feature, narrow, 1))
    kv_rows = jnp.concatenate(out_kv)
    q_rows = jnp.concatenate(out_q)
    sh_rows = jnp.concatenate(out_sh)

    my_lengths = lax.dynamic_index_in_dim(lengths, row_index, 0, keepdims=False)
    my_picked = lax.dynamic_slice_in_dim(selected, row_index * req_here, req_here, 0)
    token_place = jnp.arange(token_span, dtype=jnp.int32)
    keyval = kv_rows[row_of].reshape(req_here, token_span, 2, narrow)
    alive = token_place[None, :] < (my_lengths * group_len)[:, None]
    joined_cache = jnp.where(alive[:, :, None, None], keyval, jnp.zeros_like(keyval))

    req_ids = jnp.arange(req_here, dtype=jnp.int32)[:, None]
    picked_row = row_of.reshape(req_here, token_span)[req_ids, my_picked]
    queries = q_rows[picked_row]
    picked_shift = sh_rows[picked_row]

    feature_head = (first_feature + jnp.arange(narrow, dtype=jnp.int32)) // HEAD_DIM
    first_head = first_feature // HEAD_DIM
    last_piece = (first_feature + narrow - 1) // HEAD_DIM - first_head
    piece_count = (narrow + 2 * HEAD_DIM - 2) // HEAD_DIM
    query_f = queries.astype(jnp.float32)
    key_f = joined_cache[:, :, 0].astype(jnp.float32)
    value_f = joined_cache[:, :, 1].astype(jnp.float32)
    masks = [feature_head == first_head + p for p in range(piece_count)]
    partial = [
        jnp.einsum(
            "bie,bte->bit", jnp.where(m[None, None, :], query_f, 0.0), key_f, precision=HIGH
        )
        for m in masks
    ]
    right_piece = partial[0]
    for p in range(1, piece_count):
        right_piece = jnp.where(last_piece == p, partial[p], right_piece)
    from_left = lax.ppermute(right_piece, "col", [(i, i + 1) for i in range(col_count - 1)])
    from_right = lax.ppermute(partial[0], "col", [(i + 1, i) for i in range(col_count - 1)])
    allowed = token_place[None, None, :] <= my_picked[:, :, None]
    attended = jnp.zeros((req_here, sel_count, narrow), jnp.float32)
    for p in range(piece_count):
        full = partial[p]
        if p == 0:
            full = full + from_left
        full = full + jnp.where(last_piece == p, from_right, 0.0)
        scores = jnp.where(allowed, full * 0.125, -1e30)
        highest = jnp.max(scores, axis=-1, keepdims=True)
        weights = jnp.where(allowed, jnp.exp(scores - highest), 0.0)
        totals = jnp.sum(weights, axis=-1)
        summed = jnp.einsum("bit,bte->bie", weights, value_f, precision=HIGH)
        attended = jnp.where(masks[p][None, None, :], summed / totals[:, :, None], attended)
    attended = attended.astype(jnp.bfloat16).reshape(query_count, narrow)

    projected = lax.dot_general(
        attended, out_rows, (((1,), (1,)), ((), ())), preferred_element_type=jnp.float32
    )
    projected = projected.reshape(query_count, col_count, narrow).transpose(1, 0, 2)
    own_out = jnp.sum(lax.all_to_all(projected, "col", 0, 0, tiled=True), axis=0)
    hidden_out = (picked_shift.reshape(query_count, narrow) + own_out).astype(jnp.bfloat16)
    return (joined_cache, hidden_out.reshape(req_here, sel_count, narrow))


def solution(mesh):
    return jax.shard_map(
        per_device,
        mesh=mesh,
        in_specs=(
            P("row", None, None),
            P(),
            P(),
            P("row", "col"),
            P("row", None, "col"),
            P("col", "row"),
            P(),
            P(),
            P(),
        ),
        out_specs=(P("row", None, None, "col"), P("row", None, "col")),
        check_vma=False,
    )
```

```python
import jax
import jax.numpy as jnp
from jax import lax
from jax.sharding import PartitionSpec as P

HEADS = 25
HEAD_DIM = 64
REM_DEV = 32
TOKEN_SPLIT = 4
HIGH = lax.Precision.HIGHEST


def layer_norm(shifted, ln_gain):
    center = shifted - jnp.mean(shifted, axis=-1, keepdims=True)
    spread = jnp.mean(center * center, axis=-1, keepdims=True)
    return center * lax.rsqrt(spread + 1e-05) * ln_gain.astype(jnp.float32)


def fetch_groups(group_store, group_src, row_count, row_index, col_count, col_index, req_here, extra):
    slot_count, group_len, full_width = group_store.shape
    group_count = group_src.shape[1]
    ref_count = req_here * group_count
    local_count = ref_count - REM_DEV
    capacity = max(2, (REM_DEV + row_count - 2) // (row_count - 1))
    owner_src = group_src.reshape(row_count, ref_count)
    holder_all = owner_src // slot_count
    slot_all = owner_src % slot_count
    owner_ids = jnp.arange(row_count, dtype=jnp.int32)
    remote_all = holder_all != owner_ids[:, None]
    outgoing = remote_all & (holder_all == row_index)
    out_rank = jnp.cumsum(outgoing.astype(jnp.int32), axis=1) - 1
    slot_ids = jnp.arange(capacity, dtype=jnp.int32)
    chosen = outgoing[:, None, :] & (out_rank[:, None, :] == slot_ids[None, :, None])
    send_slot = jnp.sum(jnp.where(chosen, slot_all[:, None, :], 0), axis=2)
    send_live = jnp.any(chosen, axis=2)
    my_holder = lax.dynamic_index_in_dim(holder_all, row_index, 0, keepdims=False)
    my_slot = lax.dynamic_index_in_dim(slot_all, row_index, 0, keepdims=False)
    my_remote = lax.dynamic_index_in_dim(remote_all, row_index, 0, keepdims=False)
    incoming = (my_holder[None, :] == owner_ids[:, None]) & my_remote[None, :]
    in_rank = jnp.cumsum(incoming.astype(jnp.int32), axis=1) - 1
    my_rank = jnp.sum(jnp.where(incoming, in_rank, 0), axis=0)
    flat_index = my_holder * capacity + my_rank
    ordinal = jnp.cumsum(my_remote.astype(jnp.int32)) - 1
    compact_ids = jnp.arange(REM_DEV, dtype=jnp.int32)
    compact_pick = my_remote[None, :] & (ordinal[None, :] == compact_ids[:, None])
    compact_index = jnp.sum(jnp.where(compact_pick, flat_index[None, :], 0), axis=1)
    compact_ref = jnp.sum(jnp.where(compact_pick, jnp.arange(ref_count)[None, :], 0), axis=1)
    local_ordinal = jnp.cumsum((~my_remote).astype(jnp.int32)) - 1
    local_ids = jnp.arange(local_count, dtype=jnp.int32)
    local_pick = (~my_remote)[None, :] & (local_ordinal[None, :] == local_ids[:, None])
    local_ref = jnp.sum(jnp.where(local_pick, jnp.arange(ref_count)[None, :], 0), axis=1)
    local_slot = jnp.sum(jnp.where(local_pick, my_slot[None, :], 0), axis=1)

    split = TOKEN_SPLIT
    if col_count % split or group_len % split:
        split = 1
    part = group_len // split
    own_part = col_index % split
    store_rows = group_store.reshape(slot_count * group_len, full_width)
    tok_ids = jnp.arange(part, dtype=jnp.int32)
    send_rows = send_slot[:, :, None] * group_len + own_part * part + tok_ids
    payload = store_rows[send_rows.reshape(-1)].reshape(row_count, capacity * part, full_width)
    live_rows = jnp.repeat(send_live, part, axis=1)
    sent = jnp.where(live_rows[:, :, None], payload, jnp.zeros_like(payload))
    received = lax.all_to_all(sent, "row", split_axis=0, concat_axis=0, tiled=True)
    extra, received = lax.optimization_barrier((extra, received))
    extra_tiles = extra.reshape(16, -1)
    extra_all = lax.all_to_all(
        jnp.broadcast_to(extra_tiles[None], (row_count,) + extra_tiles.shape), "row", 0, 0, tiled=True
    ).reshape((row_count,) + extra.shape)
    flat = received.reshape(row_count * capacity * part, full_width)
    compact = flat[(compact_index[:, None] * part + tok_ids).reshape(-1)]
    pieces = [compact] + [
        lax.ppermute(compact, "col", [(c, c ^ m) for c in range(col_count)]) for m in range(1, split)
    ]
    near_rows = (local_slot[:, None] * group_len + jnp.arange(group_len, dtype=jnp.int32)).reshape(-1)
    near = store_rows[near_rows]
    blocks = [near]
    refs = [jnp.repeat(local_ref, group_len)]
    toks = [(0, group_len)]
    for m in range(split):
        blocks.append(pieces[m])
        refs.append(jnp.repeat(compact_ref, part))
        toks.append(((own_part ^ m) * part, part))
    tok_all = jnp.arange(group_len, dtype=jnp.int32)[None, :]
    remote_row = local_count * group_len + (
        ((tok_all // part) ^ own_part) * REM_DEV * part + ordinal[:, None] * part + tok_all % part
    )
    near_row = local_ordinal[:, None] * group_len + tok_all
    row_of = jnp.where(my_remote[:, None], remote_row, near_row)
    return blocks, refs, toks, row_of.reshape(-1), extra_all


def per_device(
    group_store, positions, ln_gain, w_query, w_keyval, w_out, group_src, lengths, selected
):
    row_count = lax.axis_size("row")
    col_count = lax.axis_size("col")
    row_index = lax.axis_index("row")
    col_index = lax.axis_index("col")
    slot_count, group_len, full_width = group_store.shape
    narrow = full_width // col_count
    req_here = lengths.shape[1]
    group_count = group_src.shape[1]
    token_span = group_count * group_len
    sel_count = selected.shape[1]
    query_count = req_here * sel_count
    first_feature = col_index * narrow

    pack = jnp.concatenate(
        [w_keyval.reshape(w_keyval.shape[0], 2 * narrow), w_query, w_out.T], axis=1
    )
    blocks, refs, toks, row_of, allw = fetch_groups(
        group_store, group_src, row_count, row_index, col_count, col_index, req_here, pack
    )
    allw = allw.reshape(full_width, 4 * narrow)
    w_cat = allw[:, : 3 * narrow]
    out_rows = allw[:, 3 * narrow:]

    out_kv, out_q, out_sh = [], [], []
    for block, ref, (tok_start, tok_len) in zip(blocks, refs, toks):
        groups_in = block.shape[0] // tok_len
        tok = tok_start + jnp.tile(jnp.arange(tok_len, dtype=jnp.int32), groups_in)
        place = (ref % group_count) * group_len + tok
        pos_place = positions[place].astype(jnp.float32)
        pos_tok = lax.dynamic_slice_in_dim(positions, tok_start, tok_len, 0).astype(jnp.float32)
        pos_tok = jnp.broadcast_to(pos_tok[None], (groups_in, tok_len, full_width)).reshape(block.shape)
        shifted = block.astype(jnp.float32) + pos_place - pos_tok
        normed = layer_norm(shifted, ln_gain).astype(jnp.bfloat16)
        both = jnp.dot(normed, w_cat, preferred_element_type=jnp.float32).astype(jnp.bfloat16)
        out_kv.append(both[:, : 2 * narrow])
        out_q.append(both[:, 2 * narrow:])
        out_sh.append(lax.dynamic_slice_in_dim(shifted, first_feature, narrow, 1))
    kv_rows = jnp.concatenate(out_kv)
    q_rows = jnp.concatenate(out_q)
    sh_rows = jnp.concatenate(out_sh)

    my_lengths = lax.dynamic_index_in_dim(lengths, row_index, 0, keepdims=False)
    my_picked = lax.dynamic_slice_in_dim(selected, row_index * req_here, req_here, 0)
    token_place = jnp.arange(token_span, dtype=jnp.int32)
    keyval = kv_rows[row_of].reshape(req_here, token_span, 2, narrow)
    alive = token_place[None, :] < (my_lengths * group_len)[:, None]
    joined_cache = jnp.where(alive[:, :, None, None], keyval, jnp.zeros_like(keyval))

    req_ids = jnp.arange(req_here, dtype=jnp.int32)[:, None]
    picked_row = row_of.reshape(req_here, token_span)[req_ids, my_picked]
    queries = q_rows[picked_row]
    picked_shift = sh_rows[picked_row]

    feature_head = (first_feature + jnp.arange(narrow, dtype=jnp.int32)) // HEAD_DIM
    first_head = first_feature // HEAD_DIM
    last_piece = (first_feature + narrow - 1) // HEAD_DIM - first_head
    piece_count = (narrow + 2 * HEAD_DIM - 2) // HEAD_DIM
    query_f = queries.astype(jnp.float32)
    key_f = joined_cache[:, :, 0].astype(jnp.float32)
    value_f = joined_cache[:, :, 1].astype(jnp.float32)
    masks = [feature_head == first_head + p for p in range(piece_count)]
    partial = [
        jnp.einsum(
            "bie,bte->bit", jnp.where(m[None, None, :], query_f, 0.0), key_f, precision=HIGH
        )
        for m in masks
    ]
    right_piece = partial[0]
    for p in range(1, piece_count):
        right_piece = jnp.where(last_piece == p, partial[p], right_piece)
    from_left = lax.ppermute(right_piece, "col", [(i, i + 1) for i in range(col_count - 1)])
    from_right = lax.ppermute(partial[0], "col", [(i + 1, i) for i in range(col_count - 1)])
    allowed = token_place[None, None, :] <= my_picked[:, :, None]
    attended = jnp.zeros((req_here, sel_count, narrow), jnp.float32)
    for p in range(piece_count):
        full = partial[p]
        if p == 0:
            full = full + from_left
        full = full + jnp.where(last_piece == p, from_right, 0.0)
        scores = jnp.where(allowed, full * 0.125, -1e30)
        highest = jnp.max(scores, axis=-1, keepdims=True)
        weights = jnp.where(allowed, jnp.exp(scores - highest), 0.0)
        totals = jnp.sum(weights, axis=-1)
        summed = jnp.einsum("bit,bte->bie", weights, value_f, precision=HIGH)
        attended = jnp.where(masks[p][None, None, :], summed / totals[:, :, None], attended)
    attended = attended.astype(jnp.bfloat16).reshape(query_count, narrow)

    projected = lax.dot_general(
        attended, out_rows, (((1,), (1,)), ((), ())), preferred_element_type=jnp.float32
    )
    projected = projected.reshape(query_count, col_count, narrow).transpose(1, 0, 2)
    own_out = jnp.sum(lax.all_to_all(projected, "col", 0, 0, tiled=True), axis=0)
    hidden_out = (picked_shift.reshape(query_count, narrow) + own_out).astype(jnp.bfloat16)
    return (joined_cache, hidden_out.reshape(req_here, sel_count, narrow))


def solution(mesh):
    return jax.shard_map(
        per_device,
        mesh=mesh,
        in_specs=(
            P("row", None, None),
            P(),
            P(),
            P("row", "col"),
            P("row", None, "col"),
            P("col", "row"),
            P(),
            P(),
            P(),
        ),
        out_specs=(P("row", None, None, "col"), P("row", None, "col")),
        check_vma=False,
    )
```

```python
import jax
import jax.numpy as jnp
from jax import lax
from jax.sharding import PartitionSpec as P

HEADS = 25
HEAD_DIM = 64
REM_DEV = 32
TOKEN_SPLIT = 8
HIGH = lax.Precision.HIGHEST


def layer_norm(shifted, ln_gain):
    center = shifted - jnp.mean(shifted, axis=-1, keepdims=True)
    spread = jnp.mean(center * center, axis=-1, keepdims=True)
    return center * lax.rsqrt(spread + 1e-05) * ln_gain.astype(jnp.float32)


def fetch_groups(group_store, group_src, row_count, row_index, col_count, col_index, req_here, extra):
    slot_count, group_len, full_width = group_store.shape
    group_count = group_src.shape[1]
    ref_count = req_here * group_count
    local_count = ref_count - REM_DEV
    capacity = max(2, (REM_DEV + row_count - 2) // (row_count - 1))
    owner_src = group_src.reshape(row_count, ref_count)
    holder_all = owner_src // slot_count
    slot_all = owner_src % slot_count
    owner_ids = jnp.arange(row_count, dtype=jnp.int32)
    remote_all = holder_all != owner_ids[:, None]
    outgoing = remote_all & (holder_all == row_index)
    out_rank = jnp.cumsum(outgoing.astype(jnp.int32), axis=1) - 1
    slot_ids = jnp.arange(capacity, dtype=jnp.int32)
    chosen = outgoing[:, None, :] & (out_rank[:, None, :] == slot_ids[None, :, None])
    send_slot = jnp.sum(jnp.where(chosen, slot_all[:, None, :], 0), axis=2)
    send_live = jnp.any(chosen, axis=2)
    my_holder = lax.dynamic_index_in_dim(holder_all, row_index, 0, keepdims=False)
    my_slot = lax.dynamic_index_in_dim(slot_all, row_index, 0, keepdims=False)
    my_remote = lax.dynamic_index_in_dim(remote_all, row_index, 0, keepdims=False)
    incoming = (my_holder[None, :] == owner_ids[:, None]) & my_remote[None, :]
    in_rank = jnp.cumsum(incoming.astype(jnp.int32), axis=1) - 1
    my_rank = jnp.sum(jnp.where(incoming, in_rank, 0), axis=0)
    flat_index = my_holder * capacity + my_rank
    ordinal = jnp.cumsum(my_remote.astype(jnp.int32)) - 1
    compact_ids = jnp.arange(REM_DEV, dtype=jnp.int32)
    compact_pick = my_remote[None, :] & (ordinal[None, :] == compact_ids[:, None])
    compact_index = jnp.sum(jnp.where(compact_pick, flat_index[None, :], 0), axis=1)
    compact_ref = jnp.sum(jnp.where(compact_pick, jnp.arange(ref_count)[None, :], 0), axis=1)
    local_ordinal = jnp.cumsum((~my_remote).astype(jnp.int32)) - 1
    local_ids = jnp.arange(local_count, dtype=jnp.int32)
    local_pick = (~my_remote)[None, :] & (local_ordinal[None, :] == local_ids[:, None])
    local_ref = jnp.sum(jnp.where(local_pick, jnp.arange(ref_count)[None, :], 0), axis=1)
    local_slot = jnp.sum(jnp.where(local_pick, my_slot[None, :], 0), axis=1)

    split = TOKEN_SPLIT
    if col_count % split or group_len % split:
        split = 1
    part = group_len // split
    own_part = col_index % split
    store_rows = group_store.reshape(slot_count * group_len, full_width)
    tok_ids = jnp.arange(part, dtype=jnp.int32)
    row_split = max(1, 16 // (capacity * part))
    if full_width % row_split:
        row_split = 1
    seg = full_width // row_split
    seg_ids = jnp.arange(row_split, dtype=jnp.int32)
    store_segs = group_store.reshape(slot_count * group_len * row_split, seg)
    send_rows = (send_slot[:, :, None] * group_len + own_part * part + tok_ids)[..., None] * row_split + seg_ids
    payload = store_segs[send_rows.reshape(-1)].reshape(row_count, capacity * part * row_split, seg)
    live_rows = jnp.repeat(send_live, part * row_split, axis=1)
    sent = jnp.where(live_rows[:, :, None], payload, jnp.zeros_like(payload))
    received = lax.all_to_all(sent, "row", split_axis=0, concat_axis=0, tiled=True)
    extra, received = lax.optimization_barrier((extra, received))
    extra_tiles = extra.reshape(16, -1)
    extra_all = lax.all_to_all(
        jnp.broadcast_to(extra_tiles[None], (row_count,) + extra_tiles.shape), "row", 0, 0, tiled=True
    ).reshape((row_count,) + extra.shape)
    flat = received.reshape(row_count * capacity * part * row_split, seg)
    compact_rows = (compact_index[:, None] * part + tok_ids)[..., None] * row_split + seg_ids
    compact = flat[compact_rows.reshape(-1)].reshape(REM_DEV * part, full_width)
    pieces = [compact] + [
        lax.ppermute(compact, "col", [(c, c ^ m) for c in range(col_count)]) for m in range(1, split)
    ]
    near_rows = (local_slot[:, None] * group_len + jnp.arange(group_len, dtype=jnp.int32)).reshape(-1)
    near = store_rows[near_rows]
    blocks = [near]
    refs = [jnp.repeat(local_ref, group_len)]
    toks = [(0, group_len)]
    for m in range(split):
        blocks.append(pieces[m])
        refs.append(jnp.repeat(compact_ref, part))
        toks.append(((own_part ^ m) * part, part))
    tok_all = jnp.arange(group_len, dtype=jnp.int32)[None, :]
    remote_row = local_count * group_len + (
        ((tok_all // part) ^ own_part) * REM_DEV * part + ordinal[:, None] * part + tok_all % part
    )
    near_row = local_ordinal[:, None] * group_len + tok_all
    row_of = jnp.where(my_remote[:, None], remote_row, near_row)
    return blocks, refs, toks, row_of.reshape(-1), extra_all


def per_device(
    group_store, positions, ln_gain, w_query, w_keyval, w_out, group_src, lengths, selected
):
    row_count = lax.axis_size("row")
    col_count = lax.axis_size("col")
    row_index = lax.axis_index("row")
    col_index = lax.axis_index("col")
    slot_count, group_len, full_width = group_store.shape
    narrow = full_width // col_count
    req_here = lengths.shape[1]
    group_count = group_src.shape[1]
    token_span = group_count * group_len
    sel_count = selected.shape[1]
    query_count = req_here * sel_count
    first_feature = col_index * narrow

    pack = jnp.concatenate(
        [w_keyval.reshape(w_keyval.shape[0], 2 * narrow), w_query, w_out.T], axis=1
    )
    blocks, refs, toks, row_of, allw = fetch_groups(
        group_store, group_src, row_count, row_index, col_count, col_index, req_here, pack
    )
    allw = allw.reshape(full_width, 4 * narrow)
    w_cat = allw[:, : 3 * narrow]
    out_rows = allw[:, 3 * narrow:]

    out_kv, out_q, out_sh = [], [], []
    for block, ref, (tok_start, tok_len) in zip(blocks, refs, toks):
        groups_in = block.shape[0] // tok_len
        tok = tok_start + jnp.tile(jnp.arange(tok_len, dtype=jnp.int32), groups_in)
        place = (ref % group_count) * group_len + tok
        pos_place = positions[place].astype(jnp.float32)
        pos_tok = lax.dynamic_slice_in_dim(positions, tok_start, tok_len, 0).astype(jnp.float32)
        pos_tok = jnp.broadcast_to(pos_tok[None], (groups_in, tok_len, full_width)).reshape(block.shape)
        shifted = block.astype(jnp.float32) + pos_place - pos_tok
        normed = layer_norm(shifted, ln_gain).astype(jnp.bfloat16)
        both = jnp.dot(normed, w_cat, preferred_element_type=jnp.float32).astype(jnp.bfloat16)
        out_kv.append(both[:, : 2 * narrow])
        out_q.append(both[:, 2 * narrow:])
        out_sh.append(lax.dynamic_slice_in_dim(shifted, first_feature, narrow, 1))
    kv_rows = jnp.concatenate(out_kv)
    q_rows = jnp.concatenate(out_q)
    sh_rows = jnp.concatenate(out_sh)

    my_lengths = lax.dynamic_index_in_dim(lengths, row_index, 0, keepdims=False)
    my_picked = lax.dynamic_slice_in_dim(selected, row_index * req_here, req_here, 0)
    token_place = jnp.arange(token_span, dtype=jnp.int32)
    keyval = kv_rows[row_of].reshape(req_here, token_span, 2, narrow)
    alive = token_place[None, :] < (my_lengths * group_len)[:, None]
    joined_cache = jnp.where(alive[:, :, None, None], keyval, jnp.zeros_like(keyval))

    req_ids = jnp.arange(req_here, dtype=jnp.int32)[:, None]
    picked_row = row_of.reshape(req_here, token_span)[req_ids, my_picked]
    queries = q_rows[picked_row]
    picked_shift = sh_rows[picked_row]

    feature_head = (first_feature + jnp.arange(narrow, dtype=jnp.int32)) // HEAD_DIM
    first_head = first_feature // HEAD_DIM
    last_piece = (first_feature + narrow - 1) // HEAD_DIM - first_head
    piece_count = (narrow + 2 * HEAD_DIM - 2) // HEAD_DIM
    query_f = queries.astype(jnp.float32)
    key_f = joined_cache[:, :, 0].astype(jnp.float32)
    value_f = joined_cache[:, :, 1].astype(jnp.float32)
    masks = [feature_head == first_head + p for p in range(piece_count)]
    partial = [
        jnp.einsum(
            "bie,bte->bit", jnp.where(m[None, None, :], query_f, 0.0), key_f, precision=HIGH
        )
        for m in masks
    ]
    right_piece = partial[0]
    for p in range(1, piece_count):
        right_piece = jnp.where(last_piece == p, partial[p], right_piece)
    from_left = lax.ppermute(right_piece, "col", [(i, i + 1) for i in range(col_count - 1)])
    from_right = lax.ppermute(partial[0], "col", [(i + 1, i) for i in range(col_count - 1)])
    allowed = token_place[None, None, :] <= my_picked[:, :, None]
    attended = jnp.zeros((req_here, sel_count, narrow), jnp.float32)
    for p in range(piece_count):
        full = partial[p]
        if p == 0:
            full = full + from_left
        full = full + jnp.where(last_piece == p, from_right, 0.0)
        scores = jnp.where(allowed, full * 0.125, -1e30)
        highest = jnp.max(scores, axis=-1, keepdims=True)
        weights = jnp.where(allowed, jnp.exp(scores - highest), 0.0)
        totals = jnp.sum(weights, axis=-1)
        summed = jnp.einsum("bit,bte->bie", weights, value_f, precision=HIGH)
        attended = jnp.where(masks[p][None, None, :], summed / totals[:, :, None], attended)
    attended = attended.astype(jnp.bfloat16).reshape(query_count, narrow)

    projected = lax.dot_general(
        attended, out_rows, (((1,), (1,)), ((), ())), preferred_element_type=jnp.float32
    )
    projected = projected.reshape(query_count, col_count, narrow).transpose(1, 0, 2)
    own_out = jnp.sum(lax.all_to_all(projected, "col", 0, 0, tiled=True), axis=0)
    hidden_out = (picked_shift.reshape(query_count, narrow) + own_out).astype(jnp.bfloat16)
    return (joined_cache, hidden_out.reshape(req_here, sel_count, narrow))


def solution(mesh):
    return jax.shard_map(
        per_device,
        mesh=mesh,
        in_specs=(
            P("row", None, None),
            P(),
            P(),
            P("row", "col"),
            P("row", None, "col"),
            P("col", "row"),
            P(),
            P(),
            P(),
        ),
        out_specs=(P("row", None, None, "col"), P("row", None, "col")),
        check_vma=False,
    )
```

```python
import jax
import jax.numpy as jnp
from jax import lax
from jax.sharding import PartitionSpec as P

HEADS = 25
HEAD_DIM = 64
REM_DEV = 32
TOKEN_SPLIT = 4
HIGH = lax.Precision.HIGHEST


def layer_norm(shifted, ln_gain):
    center = shifted - jnp.mean(shifted, axis=-1, keepdims=True)
    spread = jnp.mean(center * center, axis=-1, keepdims=True)
    return center * lax.rsqrt(spread + 1e-05) * ln_gain.astype(jnp.float32)


def fetch_groups(group_store, group_src, row_count, row_index, col_count, col_index, req_here, extra):
    slot_count, group_len, full_width = group_store.shape
    group_count = group_src.shape[1]
    ref_count = req_here * group_count
    local_count = ref_count - REM_DEV
    capacity = max(2, (REM_DEV + row_count - 2) // (row_count - 1))
    owner_src = group_src.reshape(row_count, ref_count)
    holder_all = owner_src // slot_count
    slot_all = owner_src % slot_count
    owner_ids = jnp.arange(row_count, dtype=jnp.int32)
    remote_all = holder_all != owner_ids[:, None]
    outgoing = remote_all & (holder_all == row_index)
    out_rank = jnp.cumsum(outgoing.astype(jnp.int32), axis=1) - 1
    slot_ids = jnp.arange(capacity, dtype=jnp.int32)
    chosen = outgoing[:, None, :] & (out_rank[:, None, :] == slot_ids[None, :, None])
    send_slot = jnp.sum(jnp.where(chosen, slot_all[:, None, :], 0), axis=2)
    send_live = jnp.any(chosen, axis=2)
    my_holder = lax.dynamic_index_in_dim(holder_all, row_index, 0, keepdims=False)
    my_slot = lax.dynamic_index_in_dim(slot_all, row_index, 0, keepdims=False)
    my_remote = lax.dynamic_index_in_dim(remote_all, row_index, 0, keepdims=False)
    incoming = (my_holder[None, :] == owner_ids[:, None]) & my_remote[None, :]
    in_rank = jnp.cumsum(incoming.astype(jnp.int32), axis=1) - 1
    my_rank = jnp.sum(jnp.where(incoming, in_rank, 0), axis=0)
    flat_index = my_holder * capacity + my_rank
    ordinal = jnp.cumsum(my_remote.astype(jnp.int32)) - 1
    compact_ids = jnp.arange(REM_DEV, dtype=jnp.int32)
    compact_pick = my_remote[None, :] & (ordinal[None, :] == compact_ids[:, None])
    compact_index = jnp.sum(jnp.where(compact_pick, flat_index[None, :], 0), axis=1)
    compact_ref = jnp.sum(jnp.where(compact_pick, jnp.arange(ref_count)[None, :], 0), axis=1)
    local_ordinal = jnp.cumsum((~my_remote).astype(jnp.int32)) - 1
    local_ids = jnp.arange(local_count, dtype=jnp.int32)
    local_pick = (~my_remote)[None, :] & (local_ordinal[None, :] == local_ids[:, None])
    local_ref = jnp.sum(jnp.where(local_pick, jnp.arange(ref_count)[None, :], 0), axis=1)
    local_slot = jnp.sum(jnp.where(local_pick, my_slot[None, :], 0), axis=1)

    split = TOKEN_SPLIT
    if col_count % split or group_len % split:
        split = 1
    part = group_len // split
    own_part = col_index % split
    store_rows = group_store.reshape(slot_count * group_len, full_width)
    tok_ids = jnp.arange(part, dtype=jnp.int32)
    send_rows = send_slot[:, :, None] * group_len + own_part * part + tok_ids
    payload = store_rows[send_rows.reshape(-1)].reshape(row_count, capacity * part, full_width)
    live_rows = jnp.repeat(send_live, part, axis=1)
    sent = jnp.where(live_rows[:, :, None], payload, jnp.zeros_like(payload))
    received = lax.all_to_all(sent, "row", split_axis=0, concat_axis=0, tiled=True)
    extra, received = lax.optimization_barrier((extra, received))
    extra_tiles = extra.reshape(16, -1)
    extra_all = lax.all_to_all(
        jnp.broadcast_to(extra_tiles[None], (row_count,) + extra_tiles.shape), "row", 0, 0, tiled=True
    ).reshape((row_count,) + extra.shape)
    flat = received.reshape(row_count * capacity * part, full_width)
    compact = flat[(compact_index[:, None] * part + tok_ids).reshape(-1)]
    pieces = [compact] + [
        lax.ppermute(compact, "col", [(c, c ^ m) for c in range(col_count)]) for m in range(1, split)
    ]
    near_rows = (local_slot[:, None] * group_len + jnp.arange(group_len, dtype=jnp.int32)).reshape(-1)
    near = store_rows[near_rows]
    blocks = [near]
    refs = [jnp.repeat(local_ref, group_len)]
    toks = [(0, group_len)]
    for m in range(split):
        blocks.append(pieces[m])
        refs.append(jnp.repeat(compact_ref, part))
        toks.append(((own_part ^ m) * part, part))
    tok_all = jnp.arange(group_len, dtype=jnp.int32)[None, :]
    remote_row = local_count * group_len + (
        ((tok_all // part) ^ own_part) * REM_DEV * part + ordinal[:, None] * part + tok_all % part
    )
    near_row = local_ordinal[:, None] * group_len + tok_all
    row_of = jnp.where(my_remote[:, None], remote_row, near_row)
    return blocks, refs, toks, row_of.reshape(-1), extra_all


def per_device(
    group_store, positions, ln_gain, w_query, w_keyval, w_out, group_src, lengths, selected
):
    row_count = lax.axis_size("row")
    col_count = lax.axis_size("col")
    row_index = lax.axis_index("row")
    col_index = lax.axis_index("col")
    slot_count, group_len, full_width = group_store.shape
    narrow = full_width // col_count
    req_here = lengths.shape[1]
    group_count = group_src.shape[1]
    token_span = group_count * group_len
    sel_count = selected.shape[1]
    query_count = req_here * sel_count
    first_feature = col_index * narrow

    pack = jnp.concatenate(
        [w_keyval.reshape(w_keyval.shape[0], 2 * narrow), w_query, w_out.T], axis=1
    )
    blocks, refs, toks, row_of, allw = fetch_groups(
        group_store, group_src, row_count, row_index, col_count, col_index, req_here, pack
    )
    allw = allw.reshape(full_width, 4 * narrow)
    w_cat = allw[:, : 3 * narrow]
    out_rows = allw[:, 3 * narrow:]

    out_kv, out_q, out_sh = [], [], []
    for block, ref, (tok_start, tok_len) in zip(blocks, refs, toks):
        groups_in = block.shape[0] // tok_len
        tok = tok_start + jnp.tile(jnp.arange(tok_len, dtype=jnp.int32), groups_in)
        place = (ref % group_count) * group_len + tok
        pos_place = positions[place].astype(jnp.float32)
        pos_tok = lax.dynamic_slice_in_dim(positions, tok_start, tok_len, 0).astype(jnp.float32)
        pos_tok = jnp.broadcast_to(pos_tok[None], (groups_in, tok_len, full_width)).reshape(block.shape)
        shifted = block.astype(jnp.float32) + pos_place - pos_tok
        normed = layer_norm(shifted, ln_gain).astype(jnp.bfloat16)
        both = jnp.dot(normed, w_cat, preferred_element_type=jnp.float32).astype(jnp.bfloat16)
        out_kv.append(both[:, : 2 * narrow])
        out_q.append(both[:, 2 * narrow:])
        out_sh.append(lax.dynamic_slice_in_dim(shifted, first_feature, narrow, 1))
    kv_rows = jnp.concatenate(out_kv)
    q_rows = jnp.concatenate(out_q)
    sh_rows = jnp.concatenate(out_sh)

    my_lengths = lax.dynamic_index_in_dim(lengths, row_index, 0, keepdims=False)
    my_picked = lax.dynamic_slice_in_dim(selected, row_index * req_here, req_here, 0)
    token_place = jnp.arange(token_span, dtype=jnp.int32)
    keyval = kv_rows[row_of].reshape(req_here, token_span, 2, narrow)
    alive = token_place[None, :] < (my_lengths * group_len)[:, None]
    joined_cache = jnp.where(alive[:, :, None, None], keyval, jnp.zeros_like(keyval))

    req_ids = jnp.arange(req_here, dtype=jnp.int32)[:, None]
    picked_row = row_of.reshape(req_here, token_span)[req_ids, my_picked]
    queries = q_rows[picked_row]
    picked_shift = sh_rows[picked_row]

    feature_head = (first_feature + jnp.arange(narrow, dtype=jnp.int32)) // HEAD_DIM
    first_head = first_feature // HEAD_DIM
    last_piece = (first_feature + narrow - 1) // HEAD_DIM - first_head
    piece_count = (narrow + 2 * HEAD_DIM - 2) // HEAD_DIM
    query_f = queries.astype(jnp.float32)
    key_f = joined_cache[:, :, 0].astype(jnp.float32)
    value_f = joined_cache[:, :, 1].astype(jnp.float32)
    masks = [feature_head == first_head + p for p in range(piece_count)]
    partial = [
        jnp.einsum(
            "bie,bte->bit", jnp.where(m[None, None, :], query_f, 0.0), key_f, precision=HIGH
        )
        for m in masks
    ]
    right_piece = partial[0]
    for p in range(1, piece_count):
        right_piece = jnp.where(last_piece == p, partial[p], right_piece)
    from_left = lax.ppermute(right_piece, "col", [(i, i + 1) for i in range(col_count - 1)])
    from_right = lax.ppermute(partial[0], "col", [(i + 1, i) for i in range(col_count - 1)])
    allowed = token_place[None, None, :] <= my_picked[:, :, None]
    attended = jnp.zeros((req_here, sel_count, narrow), jnp.float32)
    for p in range(piece_count):
        full = partial[p]
        if p == 0:
            full = full + from_left
        full = full + jnp.where(last_piece == p, from_right, 0.0)
        scores = jnp.where(allowed, full * 0.125, -1e30)
        highest = jnp.max(scores, axis=-1, keepdims=True)
        weights = jnp.where(allowed, jnp.exp(scores - highest), 0.0)
        totals = jnp.sum(weights, axis=-1)
        summed = jnp.einsum("bit,bte->bie", weights, value_f, precision=HIGH)
        attended = jnp.where(masks[p][None, None, :], summed / totals[:, :, None], attended)
    attended = attended.astype(jnp.bfloat16).reshape(query_count, narrow)

    projected = lax.dot_general(
        attended, out_rows, (((1,), (1,)), ((), ())), preferred_element_type=jnp.float32
    )
    projected = projected.reshape(query_count, col_count, narrow).transpose(1, 0, 2)
    parts = lax.all_to_all(projected.astype(jnp.bfloat16), "col", 0, 0, tiled=True)
    own_out = jnp.sum(parts.astype(jnp.float32), axis=0)
    hidden_out = (picked_shift.reshape(query_count, narrow) + own_out).astype(jnp.bfloat16)
    return (joined_cache, hidden_out.reshape(req_here, sel_count, narrow))


def solution(mesh):
    return jax.shard_map(
        per_device,
        mesh=mesh,
        in_specs=(
            P("row", None, None),
            P(),
            P(),
            P("row", "col"),
            P("row", None, "col"),
            P("col", "row"),
            P(),
            P(),
            P(),
        ),
        out_specs=(P("row", None, None, "col"), P("row", None, "col")),
        check_vma=False,
    )
```

```python
import jax
import jax.numpy as jnp
from jax import lax
from jax.sharding import PartitionSpec as P

HEADS = 25
HEAD_DIM = 64
REM_DEV = 32
TOKEN_SPLIT = 4


def layer_norm(shifted, ln_gain):
    center = shifted - jnp.mean(shifted, axis=-1, keepdims=True)
    spread = jnp.mean(center * center, axis=-1, keepdims=True)
    return center * lax.rsqrt(spread + 1e-05) * ln_gain.astype(jnp.float32)


def fetch_groups(group_store, group_src, row_count, row_index, col_count, col_index, req_here, extra):
    slot_count, group_len, full_width = group_store.shape
    group_count = group_src.shape[1]
    ref_count = req_here * group_count
    local_count = ref_count - REM_DEV
    capacity = max(2, (REM_DEV + row_count - 2) // (row_count - 1))
    owner_src = group_src.reshape(row_count, ref_count)
    holder_all = owner_src // slot_count
    slot_all = owner_src % slot_count
    owner_ids = jnp.arange(row_count, dtype=jnp.int32)
    remote_all = holder_all != owner_ids[:, None]
    outgoing = remote_all & (holder_all == row_index)
    out_rank = jnp.cumsum(outgoing.astype(jnp.int32), axis=1) - 1
    slot_ids = jnp.arange(capacity, dtype=jnp.int32)
    chosen = outgoing[:, None, :] & (out_rank[:, None, :] == slot_ids[None, :, None])
    send_slot = jnp.sum(jnp.where(chosen, slot_all[:, None, :], 0), axis=2)
    send_live = jnp.any(chosen, axis=2)
    my_holder = lax.dynamic_index_in_dim(holder_all, row_index, 0, keepdims=False)
    my_slot = lax.dynamic_index_in_dim(slot_all, row_index, 0, keepdims=False)
    my_remote = lax.dynamic_index_in_dim(remote_all, row_index, 0, keepdims=False)
    incoming = (my_holder[None, :] == owner_ids[:, None]) & my_remote[None, :]
    in_rank = jnp.cumsum(incoming.astype(jnp.int32), axis=1) - 1
    my_rank = jnp.sum(jnp.where(incoming, in_rank, 0), axis=0)
    flat_index = my_holder * capacity + my_rank
    ordinal = jnp.cumsum(my_remote.astype(jnp.int32)) - 1
    compact_ids = jnp.arange(REM_DEV, dtype=jnp.int32)
    compact_pick = my_remote[None, :] & (ordinal[None, :] == compact_ids[:, None])
    compact_index = jnp.sum(jnp.where(compact_pick, flat_index[None, :], 0), axis=1)
    compact_ref = jnp.sum(jnp.where(compact_pick, jnp.arange(ref_count)[None, :], 0), axis=1)
    local_ordinal = jnp.cumsum((~my_remote).astype(jnp.int32)) - 1
    local_ids = jnp.arange(local_count, dtype=jnp.int32)
    local_pick = (~my_remote)[None, :] & (local_ordinal[None, :] == local_ids[:, None])
    local_ref = jnp.sum(jnp.where(local_pick, jnp.arange(ref_count)[None, :], 0), axis=1)
    local_slot = jnp.sum(jnp.where(local_pick, my_slot[None, :], 0), axis=1)

    split = TOKEN_SPLIT
    if col_count % split or group_len % split:
        split = 1
    part = group_len // split
    own_part = col_index % split
    store_rows = group_store.reshape(slot_count * group_len, full_width)
    tok_ids = jnp.arange(part, dtype=jnp.int32)
    send_rows = send_slot[:, :, None] * group_len + own_part * part + tok_ids
    payload = store_rows[send_rows.reshape(-1)].reshape(row_count, capacity * part, full_width)
    live_rows = jnp.repeat(send_live, part, axis=1)
    sent = jnp.where(live_rows[:, :, None], payload, jnp.zeros_like(payload))
    received = lax.all_to_all(sent, "row", split_axis=0, concat_axis=0, tiled=True)
    extra, received = lax.optimization_barrier((extra, received))
    extra_tiles = extra.reshape(16, -1)
    extra_all = lax.all_to_all(
        jnp.broadcast_to(extra_tiles[None], (row_count,) + extra_tiles.shape), "row", 0, 0, tiled=True
    ).reshape((row_count,) + extra.shape)
    flat = received.reshape(row_count * capacity * part, full_width)
    compact = flat[(compact_index[:, None] * part + tok_ids).reshape(-1)]
    pieces = [compact] + [
        lax.ppermute(compact, "col", [(c, c ^ m) for c in range(col_count)]) for m in range(1, split)
    ]
    near_rows = (local_slot[:, None] * group_len + jnp.arange(group_len, dtype=jnp.int32)).reshape(-1)
    near = store_rows[near_rows]
    blocks = [near]
    refs = [jnp.repeat(local_ref, group_len)]
    toks = [(0, group_len)]
    for m in range(split):
        blocks.append(pieces[m])
        refs.append(jnp.repeat(compact_ref, part))
        toks.append(((own_part ^ m) * part, part))
    tok_all = jnp.arange(group_len, dtype=jnp.int32)[None, :]
    remote_row = local_count * group_len + (
        ((tok_all // part) ^ own_part) * REM_DEV * part + ordinal[:, None] * part + tok_all % part
    )
    near_row = local_ordinal[:, None] * group_len + tok_all
    row_of = jnp.where(my_remote[:, None], remote_row, near_row)
    return blocks, refs, toks, row_of.reshape(-1), extra_all


def per_device(
    group_store, positions, ln_gain, w_query, w_keyval, w_out, group_src, lengths, selected
):
    row_count = lax.axis_size("row")
    col_count = lax.axis_size("col")
    row_index = lax.axis_index("row")
    col_index = lax.axis_index("col")
    slot_count, group_len, full_width = group_store.shape
    narrow = full_width // col_count
    req_here = lengths.shape[1]
    group_count = group_src.shape[1]
    token_span = group_count * group_len
    sel_count = selected.shape[1]
    query_count = req_here * sel_count
    first_feature = col_index * narrow

    pack = jnp.concatenate(
        [w_keyval.reshape(w_keyval.shape[0], 2 * narrow), w_query, w_out.T], axis=1
    )
    blocks, refs, toks, row_of, allw = fetch_groups(
        group_store, group_src, row_count, row_index, col_count, col_index, req_here, pack
    )
    allw = allw.reshape(full_width, 4 * narrow)
    w_cat = allw[:, : 3 * narrow]
    out_rows = allw[:, 3 * narrow:]

    out_kv, out_q, out_sh = [], [], []
    for block, ref, (tok_start, tok_len) in zip(blocks, refs, toks):
        groups_in = block.shape[0] // tok_len
        tok = tok_start + jnp.tile(jnp.arange(tok_len, dtype=jnp.int32), groups_in)
        place = (ref % group_count) * group_len + tok
        pos_place = positions[place].astype(jnp.float32)
        pos_tok = lax.dynamic_slice_in_dim(positions, tok_start, tok_len, 0).astype(jnp.float32)
        pos_tok = jnp.broadcast_to(pos_tok[None], (groups_in, tok_len, full_width)).reshape(block.shape)
        shifted = block.astype(jnp.float32) + pos_place - pos_tok
        normed = layer_norm(shifted, ln_gain).astype(jnp.bfloat16)
        both = jnp.dot(normed, w_cat, preferred_element_type=jnp.float32).astype(jnp.bfloat16)
        out_kv.append(both[:, : 2 * narrow])
        out_q.append(both[:, 2 * narrow:])
        out_sh.append(lax.dynamic_slice_in_dim(shifted, first_feature, narrow, 1))
    kv_rows = jnp.concatenate(out_kv)
    q_rows = jnp.concatenate(out_q)
    sh_rows = jnp.concatenate(out_sh)

    my_lengths = lax.dynamic_index_in_dim(lengths, row_index, 0, keepdims=False)
    my_picked = lax.dynamic_slice_in_dim(selected, row_index * req_here, req_here, 0)
    token_place = jnp.arange(token_span, dtype=jnp.int32)
    keyval = kv_rows[row_of].reshape(req_here, token_span, 2, narrow)
    alive = token_place[None, :] < (my_lengths * group_len)[:, None]
    joined_cache = jnp.where(alive[:, :, None, None], keyval, jnp.zeros_like(keyval))

    req_ids = jnp.arange(req_here, dtype=jnp.int32)[:, None]
    picked_row = row_of.reshape(req_here, token_span)[req_ids, my_picked]
    queries = q_rows[picked_row]
    picked_shift = sh_rows[picked_row]

    feature_head = (first_feature + jnp.arange(narrow, dtype=jnp.int32)) // HEAD_DIM
    first_head = first_feature // HEAD_DIM
    last_piece = (first_feature + narrow - 1) // HEAD_DIM - first_head
    piece_count = (narrow + 2 * HEAD_DIM - 2) // HEAD_DIM
    query_f = queries.astype(jnp.float32)
    key_f = joined_cache[:, :, 0].astype(jnp.float32)
    value_f = joined_cache[:, :, 1].astype(jnp.float32)
    masks = [feature_head == first_head + p for p in range(piece_count)]
    partial = [
        jnp.einsum(
            "bie,bte->bit", jnp.where(m[None, None, :], query_f, 0.0), key_f
        )
        for m in masks
    ]
    right_piece = partial[0]
    for p in range(1, piece_count):
        right_piece = jnp.where(last_piece == p, partial[p], right_piece)
    from_left = lax.ppermute(right_piece, "col", [(i, i + 1) for i in range(col_count - 1)])
    from_right = lax.ppermute(partial[0], "col", [(i + 1, i) for i in range(col_count - 1)])
    allowed = token_place[None, None, :] <= my_picked[:, :, None]
    attended = jnp.zeros((req_here, sel_count, narrow), jnp.float32)
    for p in range(piece_count):
        full = partial[p]
        if p == 0:
            full = full + from_left
        full = full + jnp.where(last_piece == p, from_right, 0.0)
        scores = jnp.where(allowed, full * 0.125, -1e30)
        highest = jnp.max(scores, axis=-1, keepdims=True)
        weights = jnp.where(allowed, jnp.exp(scores - highest), 0.0)
        totals = jnp.sum(weights, axis=-1)
        summed = jnp.einsum("bit,bte->bie", weights, value_f)
        attended = jnp.where(masks[p][None, None, :], summed / totals[:, :, None], attended)
    attended = attended.astype(jnp.bfloat16).reshape(query_count, narrow)

    projected = lax.dot_general(
        attended, out_rows, (((1,), (1,)), ((), ())), preferred_element_type=jnp.float32
    )
    projected = projected.reshape(query_count, col_count, narrow).transpose(1, 0, 2)
    parts = lax.all_to_all(projected.astype(jnp.bfloat16), "col", 0, 0, tiled=True)
    own_out = jnp.sum(parts.astype(jnp.float32), axis=0)
    hidden_out = (picked_shift.reshape(query_count, narrow) + own_out).astype(jnp.bfloat16)
    return (joined_cache, hidden_out.reshape(req_here, sel_count, narrow))


def solution(mesh):
    return jax.shard_map(
        per_device,
        mesh=mesh,
        in_specs=(
            P("row", None, None),
            P(),
            P(),
            P("row", "col"),
            P("row", None, "col"),
            P("col", "row"),
            P(),
            P(),
            P(),
        ),
        out_specs=(P("row", None, None, "col"), P("row", None, "col")),
        check_vma=False,
    )
```

```python
import jax
import jax.numpy as jnp
from jax import lax
from jax.sharding import PartitionSpec as P

HEADS = 25
HEAD_DIM = 64
REM_DEV = 32
TOKEN_SPLIT = 4


def layer_norm(shifted, ln_gain):
    center = shifted - jnp.mean(shifted, axis=-1, keepdims=True)
    spread = jnp.mean(center * center, axis=-1, keepdims=True)
    return center * lax.rsqrt(spread + 1e-05) * ln_gain.astype(jnp.float32)


def fetch_groups(group_store, group_src, row_count, row_index, col_count, col_index, req_here, extra):
    slot_count, group_len, full_width = group_store.shape
    group_count = group_src.shape[1]
    ref_count = req_here * group_count
    local_count = ref_count - REM_DEV
    capacity = max(2, (REM_DEV + row_count - 2) // (row_count - 1))
    owner_src = group_src.reshape(row_count, ref_count)
    holder_all = owner_src // slot_count
    slot_all = owner_src % slot_count
    owner_ids = jnp.arange(row_count, dtype=jnp.int32)
    remote_all = holder_all != owner_ids[:, None]
    outgoing = remote_all & (holder_all == row_index)
    out_rank = jnp.cumsum(outgoing.astype(jnp.int32), axis=1) - 1
    slot_ids = jnp.arange(capacity, dtype=jnp.int32)
    chosen = outgoing[:, None, :] & (out_rank[:, None, :] == slot_ids[None, :, None])
    send_slot = jnp.sum(jnp.where(chosen, slot_all[:, None, :], 0), axis=2)
    send_live = jnp.any(chosen, axis=2)
    my_holder = lax.dynamic_index_in_dim(holder_all, row_index, 0, keepdims=False)
    my_slot = lax.dynamic_index_in_dim(slot_all, row_index, 0, keepdims=False)
    my_remote = lax.dynamic_index_in_dim(remote_all, row_index, 0, keepdims=False)
    incoming = (my_holder[None, :] == owner_ids[:, None]) & my_remote[None, :]
    in_rank = jnp.cumsum(incoming.astype(jnp.int32), axis=1) - 1
    my_rank = jnp.sum(jnp.where(incoming, in_rank, 0), axis=0)
    flat_index = my_holder * capacity + my_rank
    ordinal = jnp.cumsum(my_remote.astype(jnp.int32)) - 1
    compact_ids = jnp.arange(REM_DEV, dtype=jnp.int32)
    compact_pick = my_remote[None, :] & (ordinal[None, :] == compact_ids[:, None])
    compact_index = jnp.sum(jnp.where(compact_pick, flat_index[None, :], 0), axis=1)
    compact_ref = jnp.sum(jnp.where(compact_pick, jnp.arange(ref_count)[None, :], 0), axis=1)
    local_ordinal = jnp.cumsum((~my_remote).astype(jnp.int32)) - 1
    local_ids = jnp.arange(local_count, dtype=jnp.int32)
    local_pick = (~my_remote)[None, :] & (local_ordinal[None, :] == local_ids[:, None])
    local_ref = jnp.sum(jnp.where(local_pick, jnp.arange(ref_count)[None, :], 0), axis=1)
    local_slot = jnp.sum(jnp.where(local_pick, my_slot[None, :], 0), axis=1)

    split = TOKEN_SPLIT
    if col_count % split or group_len % split:
        split = 1
    part = group_len // split
    own_part = col_index % split
    store_rows = group_store.reshape(slot_count * group_len, full_width)
    tok_ids = jnp.arange(part, dtype=jnp.int32)
    send_rows = send_slot[:, :, None] * group_len + own_part * part + tok_ids
    payload = store_rows[send_rows.reshape(-1)].reshape(row_count, capacity * part, full_width)
    live_rows = jnp.repeat(send_live, part, axis=1)
    sent = jnp.where(live_rows[:, :, None], payload, jnp.zeros_like(payload))
    received = lax.all_to_all(sent, "row", split_axis=0, concat_axis=0, tiled=True)
    extra, received = lax.optimization_barrier((extra, received))
    extra_tiles = extra.reshape(16, -1)
    extra_all = lax.all_to_all(
        jnp.broadcast_to(extra_tiles[None], (row_count,) + extra_tiles.shape), "row", 0, 0, tiled=True
    ).reshape((row_count,) + extra.shape)
    flat = received.reshape(row_count * capacity * part, full_width)
    compact = flat[(compact_index[:, None] * part + tok_ids).reshape(-1)]
    pieces = [compact] + [
        lax.ppermute(compact, "col", [(c, c ^ m) for c in range(col_count)]) for m in range(1, split)
    ]
    near_rows = (local_slot[:, None] * group_len + jnp.arange(group_len, dtype=jnp.int32)).reshape(-1)
    near = store_rows[near_rows]
    blocks = [near]
    refs = [jnp.repeat(local_ref, group_len)]
    toks = [(0, group_len)]
    for m in range(split):
        blocks.append(pieces[m])
        refs.append(jnp.repeat(compact_ref, part))
        toks.append(((own_part ^ m) * part, part))
    tok_all = jnp.arange(group_len, dtype=jnp.int32)[None, :]
    remote_row = local_count * group_len + (
        ((tok_all // part) ^ own_part) * REM_DEV * part + ordinal[:, None] * part + tok_all % part
    )
    near_row = local_ordinal[:, None] * group_len + tok_all
    row_of = jnp.where(my_remote[:, None], remote_row, near_row)
    return blocks, refs, toks, row_of.reshape(-1), extra_all


def per_device(
    group_store, positions, ln_gain, w_query, w_keyval, w_out, group_src, lengths, selected
):
    row_count = lax.axis_size("row")
    col_count = lax.axis_size("col")
    row_index = lax.axis_index("row")
    col_index = lax.axis_index("col")
    slot_count, group_len, full_width = group_store.shape
    narrow = full_width // col_count
    req_here = lengths.shape[1]
    group_count = group_src.shape[1]
    token_span = group_count * group_len
    sel_count = selected.shape[1]
    query_count = req_here * sel_count
    first_feature = col_index * narrow

    pack = jnp.concatenate(
        [w_keyval.reshape(w_keyval.shape[0], 2 * narrow), w_query, w_out.T], axis=1
    )
    blocks, refs, toks, row_of, allw = fetch_groups(
        group_store, group_src, row_count, row_index, col_count, col_index, req_here, pack
    )
    allw = allw.reshape(full_width, 4 * narrow)
    w_cat = allw[:, : 3 * narrow]
    out_rows = allw[:, 3 * narrow:]

    out_norm, out_sh = [], []
    for block, ref, (tok_start, tok_len) in zip(blocks, refs, toks):
        groups_in = block.shape[0] // tok_len
        tok = tok_start + jnp.tile(jnp.arange(tok_len, dtype=jnp.int32), groups_in)
        place = (ref % group_count) * group_len + tok
        pos_place = positions[place].astype(jnp.float32)
        pos_tok = lax.dynamic_slice_in_dim(positions, tok_start, tok_len, 0).astype(jnp.float32)
        pos_tok = jnp.broadcast_to(pos_tok[None], (groups_in, tok_len, full_width)).reshape(block.shape)
        shifted = block.astype(jnp.float32) + pos_place - pos_tok
        out_norm.append(layer_norm(shifted, ln_gain).astype(jnp.bfloat16))
        out_sh.append(lax.dynamic_slice_in_dim(shifted, first_feature, narrow, 1))
    both = jnp.dot(
        jnp.concatenate(out_norm), w_cat, preferred_element_type=jnp.float32
    ).astype(jnp.bfloat16)
    kv_rows = both[:, : 2 * narrow]
    q_rows = both[:, 2 * narrow:]
    sh_rows = jnp.concatenate(out_sh)

    my_lengths = lax.dynamic_index_in_dim(lengths, row_index, 0, keepdims=False)
    my_picked = lax.dynamic_slice_in_dim(selected, row_index * req_here, req_here, 0)
    token_place = jnp.arange(token_span, dtype=jnp.int32)
    keyval = kv_rows[row_of].reshape(req_here, token_span, 2, narrow)
    alive = token_place[None, :] < (my_lengths * group_len)[:, None]
    joined_cache = jnp.where(alive[:, :, None, None], keyval, jnp.zeros_like(keyval))

    req_ids = jnp.arange(req_here, dtype=jnp.int32)[:, None]
    picked_row = row_of.reshape(req_here, token_span)[req_ids, my_picked]
    queries = q_rows[picked_row]
    picked_shift = sh_rows[picked_row]

    feature_head = (first_feature + jnp.arange(narrow, dtype=jnp.int32)) // HEAD_DIM
    first_head = first_feature // HEAD_DIM
    last_piece = (first_feature + narrow - 1) // HEAD_DIM - first_head
    piece_count = (narrow + 2 * HEAD_DIM - 2) // HEAD_DIM
    query_f = queries.astype(jnp.float32)
    key_f = joined_cache[:, :, 0].astype(jnp.float32)
    value_f = joined_cache[:, :, 1].astype(jnp.float32)
    masks = [feature_head == first_head + p for p in range(piece_count)]
    partial = [
        jnp.einsum(
            "bie,bte->bit", jnp.where(m[None, None, :], query_f, 0.0), key_f
        )
        for m in masks
    ]
    right_piece = partial[0]
    for p in range(1, piece_count):
        right_piece = jnp.where(last_piece == p, partial[p], right_piece)
    from_left = lax.ppermute(right_piece, "col", [(i, i + 1) for i in range(col_count - 1)])
    from_right = lax.ppermute(partial[0], "col", [(i + 1, i) for i in range(col_count - 1)])
    allowed = token_place[None, None, :] <= my_picked[:, :, None]
    attended = jnp.zeros((req_here, sel_count, narrow), jnp.float32)
    for p in range(piece_count):
        full = partial[p]
        if p == 0:
            full = full + from_left
        full = full + jnp.where(last_piece == p, from_right, 0.0)
        scores = jnp.where(allowed, full * 0.125, -1e30)
        highest = jnp.max(scores, axis=-1, keepdims=True)
        weights = jnp.where(allowed, jnp.exp(scores - highest), 0.0)
        totals = jnp.sum(weights, axis=-1)
        summed = jnp.einsum("bit,bte->bie", weights, value_f)
        attended = jnp.where(masks[p][None, None, :], summed / totals[:, :, None], attended)
    attended = attended.astype(jnp.bfloat16).reshape(query_count, narrow)

    projected = lax.dot_general(
        attended, out_rows, (((1,), (1,)), ((), ())), preferred_element_type=jnp.float32
    )
    projected = projected.reshape(query_count, col_count, narrow).transpose(1, 0, 2)
    parts = lax.all_to_all(projected.astype(jnp.bfloat16), "col", 0, 0, tiled=True)
    own_out = jnp.sum(parts.astype(jnp.float32), axis=0)
    hidden_out = (picked_shift.reshape(query_count, narrow) + own_out).astype(jnp.bfloat16)
    return (joined_cache, hidden_out.reshape(req_here, sel_count, narrow))


def solution(mesh):
    return jax.shard_map(
        per_device,
        mesh=mesh,
        in_specs=(
            P("row", None, None),
            P(),
            P(),
            P("row", "col"),
            P("row", None, "col"),
            P("col", "row"),
            P(),
            P(),
            P(),
        ),
        out_specs=(P("row", None, None, "col"), P("row", None, "col")),
        check_vma=False,
    )
```

```python
import jax
import jax.numpy as jnp
from jax import lax
from jax.sharding import PartitionSpec as P

HEADS = 25
HEAD_DIM = 64
REM_DEV = 32
TOKEN_SPLIT = 4


def layer_norm(shifted, ln_gain):
    center = shifted - jnp.mean(shifted, axis=-1, keepdims=True)
    spread = jnp.mean(center * center, axis=-1, keepdims=True)
    return center * lax.rsqrt(spread + 1e-05) * ln_gain.astype(jnp.float32)


def fetch_groups(group_store, group_src, row_count, row_index, col_count, col_index, req_here, extra):
    slot_count, group_len, full_width = group_store.shape
    group_count = group_src.shape[1]
    ref_count = req_here * group_count
    local_count = ref_count - REM_DEV
    capacity = max(2, (REM_DEV + row_count - 2) // (row_count - 1))
    owner_src = group_src.reshape(row_count, ref_count)
    holder_all = owner_src // slot_count
    slot_all = owner_src % slot_count
    owner_ids = jnp.arange(row_count, dtype=jnp.int32)
    remote_all = holder_all != owner_ids[:, None]
    outgoing = remote_all & (holder_all == row_index)
    out_rank = jnp.cumsum(outgoing.astype(jnp.int32), axis=1) - 1
    slot_ids = jnp.arange(capacity, dtype=jnp.int32)
    chosen = outgoing[:, None, :] & (out_rank[:, None, :] == slot_ids[None, :, None])
    send_slot = jnp.sum(jnp.where(chosen, slot_all[:, None, :], 0), axis=2)
    send_live = jnp.any(chosen, axis=2)
    my_holder = lax.dynamic_index_in_dim(holder_all, row_index, 0, keepdims=False)
    my_slot = lax.dynamic_index_in_dim(slot_all, row_index, 0, keepdims=False)
    my_remote = lax.dynamic_index_in_dim(remote_all, row_index, 0, keepdims=False)
    incoming = (my_holder[None, :] == owner_ids[:, None]) & my_remote[None, :]
    in_rank = jnp.cumsum(incoming.astype(jnp.int32), axis=1) - 1
    my_rank = jnp.sum(jnp.where(incoming, in_rank, 0), axis=0)
    flat_index = my_holder * capacity + my_rank
    ordinal = jnp.cumsum(my_remote.astype(jnp.int32)) - 1
    compact_ids = jnp.arange(REM_DEV, dtype=jnp.int32)
    compact_pick = my_remote[None, :] & (ordinal[None, :] == compact_ids[:, None])
    compact_index = jnp.sum(jnp.where(compact_pick, flat_index[None, :], 0), axis=1)
    compact_ref = jnp.sum(jnp.where(compact_pick, jnp.arange(ref_count)[None, :], 0), axis=1)
    local_ordinal = jnp.cumsum((~my_remote).astype(jnp.int32)) - 1
    local_ids = jnp.arange(local_count, dtype=jnp.int32)
    local_pick = (~my_remote)[None, :] & (local_ordinal[None, :] == local_ids[:, None])
    local_ref = jnp.sum(jnp.where(local_pick, jnp.arange(ref_count)[None, :], 0), axis=1)
    local_slot = jnp.sum(jnp.where(local_pick, my_slot[None, :], 0), axis=1)

    split = TOKEN_SPLIT
    if col_count % split or group_len % split:
        split = 1
    part = group_len // split
    own_part = col_index % split
    store_rows = group_store.reshape(slot_count * group_len, full_width)
    tok_ids = jnp.arange(part, dtype=jnp.int32)
    send_rows = send_slot[:, :, None] * group_len + own_part * part + tok_ids
    payload = store_rows[send_rows.reshape(-1)].reshape(row_count, capacity * part, full_width)
    live_rows = jnp.repeat(send_live, part, axis=1)
    sent = jnp.where(live_rows[:, :, None], payload, jnp.zeros_like(payload))
    received = lax.all_to_all(sent, "row", split_axis=0, concat_axis=0, tiled=True)
    extra, received = lax.optimization_barrier((extra, received))
    extra_tiles = extra.reshape(16, -1)
    extra_all = lax.all_to_all(
        jnp.broadcast_to(extra_tiles[None], (row_count,) + extra_tiles.shape), "row", 0, 0, tiled=True
    ).reshape((row_count,) + extra.shape)
    flat = received.reshape(row_count * capacity * part, full_width)
    compact = flat[(compact_index[:, None] * part + tok_ids).reshape(-1)]
    pieces = [compact] + [
        lax.ppermute(compact, "col", [(c, c ^ m) for c in range(col_count)]) for m in range(1, split)
    ]
    near_rows = (local_slot[:, None] * group_len + jnp.arange(group_len, dtype=jnp.int32)).reshape(-1)
    near = store_rows[near_rows]
    blocks = [near]
    refs = [jnp.repeat(local_ref, group_len)]
    toks = [(0, group_len)]
    for m in range(split):
        blocks.append(pieces[m])
        refs.append(jnp.repeat(compact_ref, part))
        toks.append(((own_part ^ m) * part, part))
    tok_all = jnp.arange(group_len, dtype=jnp.int32)[None, :]
    remote_row = local_count * group_len + (
        ((tok_all // part) ^ own_part) * REM_DEV * part + ordinal[:, None] * part + tok_all % part
    )
    near_row = local_ordinal[:, None] * group_len + tok_all
    row_of = jnp.where(my_remote[:, None], remote_row, near_row)
    return blocks, refs, toks, row_of.reshape(-1), extra_all


def per_device(
    group_store, positions, ln_gain, w_query, w_keyval, w_out, group_src, lengths, selected
):
    row_count = lax.axis_size("row")
    col_count = lax.axis_size("col")
    row_index = lax.axis_index("row")
    col_index = lax.axis_index("col")
    slot_count, group_len, full_width = group_store.shape
    narrow = full_width // col_count
    req_here = lengths.shape[1]
    group_count = group_src.shape[1]
    token_span = group_count * group_len
    sel_count = selected.shape[1]
    query_count = req_here * sel_count
    first_feature = col_index * narrow

    pack = jnp.concatenate(
        [w_keyval.reshape(w_keyval.shape[0], 2 * narrow), w_query, w_out.T], axis=1
    )
    blocks, refs, toks, row_of, allw = fetch_groups(
        group_store, group_src, row_count, row_index, col_count, col_index, req_here, pack
    )
    allw = allw.reshape(full_width, 4 * narrow)
    w_cat = allw[:, : 3 * narrow]
    out_rows = allw[:, 3 * narrow:]

    out_norm, out_sh = [], []
    for block, ref, (tok_start, tok_len) in zip(blocks, refs, toks):
        groups_in = block.shape[0] // tok_len
        tok = tok_start + jnp.tile(jnp.arange(tok_len, dtype=jnp.int32), groups_in)
        place = (ref % group_count) * group_len + tok
        pos_place = positions[place].astype(jnp.float32)
        pos_tok = lax.dynamic_slice_in_dim(positions, tok_start, tok_len, 0).astype(jnp.float32)
        pos_tok = jnp.broadcast_to(pos_tok[None], (groups_in, tok_len, full_width)).reshape(block.shape)
        shifted = block.astype(jnp.float32) + pos_place - pos_tok
        out_norm.append(layer_norm(shifted, ln_gain).astype(jnp.bfloat16))
        out_sh.append(lax.dynamic_slice_in_dim(shifted, first_feature, narrow, 1))
    normed_rows = jnp.concatenate(out_norm)
    sh_rows = jnp.concatenate(out_sh)

    my_lengths = lax.dynamic_index_in_dim(lengths, row_index, 0, keepdims=False)
    my_picked = lax.dynamic_slice_in_dim(selected, row_index * req_here, req_here, 0)
    token_place = jnp.arange(token_span, dtype=jnp.int32)
    keyval = jnp.dot(
        normed_rows[row_of], w_cat[:, : 2 * narrow], preferred_element_type=jnp.float32
    ).astype(jnp.bfloat16).reshape(req_here, token_span, 2, narrow)
    alive = token_place[None, :] < (my_lengths * group_len)[:, None]
    joined_cache = jnp.where(alive[:, :, None, None], keyval, jnp.zeros_like(keyval))

    req_ids = jnp.arange(req_here, dtype=jnp.int32)[:, None]
    picked_row = row_of.reshape(req_here, token_span)[req_ids, my_picked]
    queries = jnp.dot(
        normed_rows[picked_row], w_cat[:, 2 * narrow:], preferred_element_type=jnp.float32
    ).astype(jnp.bfloat16)
    picked_shift = sh_rows[picked_row]

    feature_head = (first_feature + jnp.arange(narrow, dtype=jnp.int32)) // HEAD_DIM
    first_head = first_feature // HEAD_DIM
    last_piece = (first_feature + narrow - 1) // HEAD_DIM - first_head
    piece_count = (narrow + 2 * HEAD_DIM - 2) // HEAD_DIM
    query_f = queries.astype(jnp.float32)
    key_f = joined_cache[:, :, 0].astype(jnp.float32)
    value_f = joined_cache[:, :, 1].astype(jnp.float32)
    masks = [feature_head == first_head + p for p in range(piece_count)]
    partial = [
        jnp.einsum(
            "bie,bte->bit", jnp.where(m[None, None, :], query_f, 0.0), key_f
        )
        for m in masks
    ]
    right_piece = partial[0]
    for p in range(1, piece_count):
        right_piece = jnp.where(last_piece == p, partial[p], right_piece)
    from_left = lax.ppermute(right_piece, "col", [(i, i + 1) for i in range(col_count - 1)])
    from_right = lax.ppermute(partial[0], "col", [(i + 1, i) for i in range(col_count - 1)])
    allowed = token_place[None, None, :] <= my_picked[:, :, None]
    attended = jnp.zeros((req_here, sel_count, narrow), jnp.float32)
    for p in range(piece_count):
        full = partial[p]
        if p == 0:
            full = full + from_left
        full = full + jnp.where(last_piece == p, from_right, 0.0)
        scores = jnp.where(allowed, full * 0.125, -1e30)
        highest = jnp.max(scores, axis=-1, keepdims=True)
        weights = jnp.where(allowed, jnp.exp(scores - highest), 0.0)
        totals = jnp.sum(weights, axis=-1)
        summed = jnp.einsum("bit,bte->bie", weights, value_f)
        attended = jnp.where(masks[p][None, None, :], summed / totals[:, :, None], attended)
    attended = attended.astype(jnp.bfloat16).reshape(query_count, narrow)

    projected = lax.dot_general(
        attended, out_rows, (((1,), (1,)), ((), ())), preferred_element_type=jnp.float32
    )
    projected = projected.reshape(query_count, col_count, narrow).transpose(1, 0, 2)
    parts = lax.all_to_all(projected.astype(jnp.bfloat16), "col", 0, 0, tiled=True)
    own_out = jnp.sum(parts.astype(jnp.float32), axis=0)
    hidden_out = (picked_shift.reshape(query_count, narrow) + own_out).astype(jnp.bfloat16)
    return (joined_cache, hidden_out.reshape(req_here, sel_count, narrow))


def solution(mesh):
    return jax.shard_map(
        per_device,
        mesh=mesh,
        in_specs=(
            P("row", None, None),
            P(),
            P(),
            P("row", "col"),
            P("row", None, "col"),
            P("col", "row"),
            P(),
            P(),
            P(),
        ),
        out_specs=(P("row", None, None, "col"), P("row", None, "col")),
        check_vma=False,
    )
```
